512 devices in a mesh: seq: 32 (over y, x), head: 16 (over z, core).
Axes of the slice: x: 4, y: 8, z: 8, core: 2. Of those that a mesh axis runs over, the one named last changes fastest.
Arguments:
- features: bfloat16 [65536, 8192], P(('seq', 'head')), may hold values from -6 to 6
- increment_per_head: bfloat16 [65536, 128], P(('seq', 'head')), may hold values from 0.0049743652 to 0.049804688
- token_log_decay: bfloat16 [65536, 128], P(('seq', 'head')), may hold values from -2 to 0, as said below
- b_matrix: bfloat16 [65536, 1024], P(('seq', 'head')), may hold values from -6 to 6
- c_matrix: bfloat16 [65536, 1024], P(('seq', 'head')), may hold values from -0.5 to 0.5
- skip_gain: float32 [128], P('head'), may hold values from 0.5 to 1.5
Outputs:
- mixed_out: bfloat16 [65536, 8192], P(('seq', 'head'))
The draws below stay inside these ranges and needn't reach their ends.
Inputs may be any that keep to these rules, and one draw needn't show every extreme that they name: `token_log_decay`: log decays are never positive.
All inputs are finite; a program needn't handle non-finite values.
Results may differ from the reference program's by a relative error of at most 0.01.
Values may be sent and summed in bfloat16 or wider, within the bound.
No kernel may reach another device: no remote copies, remote signals or barrier semaphores. Data moves between devices by JAX's collectives and lax.ppermute only.
A program may use at most 128 MiB of HBM per device.

```python
import math
import jax
import jax.numpy as jnp
from jax import lax

H = 128
P_SIZE = 64
N = 128
G = 8
Q = 128
TOK_DEV = 2048
TOKENS = 65536


def draw_token_log_decay(key, part):
    keys = jax.random.split(key, 5)
    fast_threshold = 8
    low_end = 0.5
    high_end = 1.5
    is_fast = jax.random.randint(keys[0], (H,), 0, 16) < fast_threshold
    base_rate = jnp.where(is_fast, 3.0 / Q, 0.5 / TOKENS)
    block_spread = jnp.exp(jax.random.uniform(keys[1], (TOKENS // TOK_DEV, 1, H), minval=-0.69, maxval=0.69))
    random_noise = jax.random.uniform(keys[2], (TOKENS // TOK_DEV, TOK_DEV, H), minval=low_end, maxval=high_end)
    element_forgetting_speed = (base_rate * block_spread * random_noise).reshape(TOKENS, H)
    sequence_offsets = jax.random.randint(keys[3], (3, 1, H), 0, TOKENS)
    hierarchy_tiers = jax.random.uniform(keys[4], (3, 1, H), minval=0.22, maxval=0.69)
    assignment_cells = jnp.arange(TOKENS, dtype=jnp.int32)[None, :, None]
    segment_extents = jnp.sum(jnp.where(assignment_cells == sequence_offsets, hierarchy_tiers, 0.0), axis=0)
    return (-(element_forgetting_speed + segment_extents)).astype(jnp.bfloat16)


def steps_of(stream_key, shape, shards, low, top_value):
    factor_of = 1.0
    for dim, shards_of in shards:
        steps = jax.random.uniform(jax.random.fold_in(jax.random.fold_in(stream_key, 6), dim), (shards_of,), jnp.float32, low / len(shards), top_value / len(shards))
        factor_of = factor_of * jnp.repeat(jnp.exp(steps), shape[dim] // shards_of).reshape((-1,) + (1,) * (len(shape) - 1 - dim))
    return factor_of


def scatter_about(own_key, dims, spread, bound, cuts=(), kind=jnp.bfloat16):
    factor_of = steps_of(own_key, dims, cuts, -0.22, 0.18) if cuts else 1.0
    result = jax.random.normal(own_key, dims, jnp.float32) * spread * factor_of
    return jnp.minimum(jnp.maximum(result, -bound), bound).astype(kind)


def setup_inputs(seed: int = 0) -> dict:
    key_of = jax.random.split(jax.random.key(seed), 7)
    return {
        "features": scatter_about(key_of[0], (TOKENS, H * P_SIZE), 1.0, 6.0, ((0, 512),)),
        "increment_per_head": jnp.clip(jnp.exp(math.log(0.049804688) - 2.3038113 * jax.random.uniform(key_of[1], (TOKENS, H), jnp.float32) ** steps_of(key_of[1], (TOKENS, H), ((0, 512),), -0.2, 0.2)), 0.0049743652, 0.049804688).astype(jnp.bfloat16),
        "token_log_decay": draw_token_log_decay(jax.random.fold_in(key_of[6], 71), 0),
        "b_matrix": scatter_about(key_of[3], (TOKENS, G * N), 1.0, 6.0, ((0, 512),)),
        "c_matrix": scatter_about(key_of[4], (TOKENS, G * N), N ** -0.5, 0.5, ((0, 512),)),
        "skip_gain": jnp.clip(0.5 + 1.0 * jax.random.uniform(key_of[5], (H,), jnp.float32) ** steps_of(key_of[5], (H,), ((0, 16),), -0.2, 0.2), 0.5, 1.5),
    }


def reference(features, increment_per_head, token_log_decay, b_matrix, c_matrix, skip_gain):
    block_count = TOKENS // Q
    group_heads = H // G

    def one_group(group_idx):
        group_x = lax.dynamic_slice_in_dim(features, group_idx * (group_heads * P_SIZE), group_heads * P_SIZE, 1)
        group_x = group_x.reshape(block_count, Q, group_heads, P_SIZE).astype(jnp.float32)
        group_step = lax.dynamic_slice_in_dim(increment_per_head, group_idx * group_heads, group_heads, 1)
        group_step = group_step.astype(jnp.float32).reshape(block_count, Q, group_heads)
        group_decay = lax.dynamic_slice_in_dim(token_log_decay, group_idx * group_heads, group_heads, 1)
        group_decay = group_decay.astype(jnp.float32).reshape(block_count, Q, group_heads)
        group_b = lax.dynamic_slice_in_dim(b_matrix, group_idx * N, N, 1).astype(jnp.float32).reshape(block_count, Q, N)
        group_c = lax.dynamic_slice_in_dim(c_matrix, group_idx * N, N, 1).astype(jnp.float32).reshape(block_count, Q, N)
        group_skip = lax.dynamic_slice_in_dim(skip_gain, group_idx * group_heads, group_heads, 0)
        within = jnp.cumsum(group_decay, axis=1)
        block_total = within[:, -1, :]
        scores = jnp.einsum('ctn,csn->cts', group_c, group_b)
        causal = (jnp.arange(Q)[:, None] >= jnp.arange(Q)[None, :])[None, :, :, None]
        gap_log = within[:, :, None, :] - within[:, None, :, :]
        damping = jnp.where(causal, jnp.exp(jnp.where(causal, gap_log, 0.0)), 0.0)
        weight = (scores[..., None] * damping * group_step[:, None, :, :]).astype(jnp.bfloat16)
        inside = jnp.einsum('ctsh,cshp->cthp', weight.astype(jnp.float32), group_x)
        factor = jnp.exp(block_total[:, None, :] - within) * group_step
        scaled = (group_x * factor[..., None]).astype(jnp.bfloat16)
        update = jnp.einsum('csn,cshp->chnp', group_b, scaled.astype(jnp.float32))

        def advance(state_now, inputs):
            total_now, update_now = inputs
            return jnp.exp(total_now)[:, None, None] * state_now + update_now, state_now

        _, carried = lax.scan(advance, jnp.zeros((group_heads, N, P_SIZE), jnp.float32), (block_total, update))
        carried_in = carried.astype(jnp.bfloat16)
        outside = jnp.einsum('ctn,chnp->cthp', group_c, carried_in.astype(jnp.float32))
        mixed = inside + jnp.exp(within)[..., None] * outside + group_skip[None, None, :, None] * group_x
        return mixed.astype(jnp.bfloat16)

    stacked = lax.map(one_group, jnp.arange(G, dtype=jnp.int32))
    return jnp.transpose(stacked, (1, 2, 0, 3, 4)).reshape(TOKENS, H * P_SIZE)
```

```python
import jax
import jax.numpy as jnp
from jax import lax
from jax.sharding import Mesh
from jax.sharding import PartitionSpec as P

G = 8
CORES = 2


def swap(value):
    return lax.ppermute(value, "core", [(0, 1), (1, 0)])


def shift_seq(value, distance, count):
    return lax.ppermute(value, "seq", [(i, i + distance) for i in range(count - distance)])


def local(features, increment_per_head, token_log_decay, b_matrix, c_matrix, skip_gain):
    f32, bf16 = jnp.float32, jnp.bfloat16
    n_seq = lax.axis_size("seq")
    n_z = lax.axis_size("z")
    n_core = lax.axis_size("core")
    z_idx = lax.axis_index("z")
    c_idx = lax.axis_index("core")
    tokens = features.shape[0]
    heads = increment_per_head.shape[1]
    width = features.shape[1] // heads
    state = b_matrix.shape[1] // G
    per_group = heads // G
    half = heads // n_core
    quarter = half // n_z

    x = features.reshape(tokens, heads, width)
    step = increment_per_head.astype(f32)
    within = jnp.cumsum(token_log_decay.astype(f32), axis=0)
    total = within[-1]
    b = b_matrix.reshape(tokens, G, state)
    c = c_matrix.reshape(tokens, G, state)
    totals = lax.all_gather(total, ("z", "core")).reshape(n_z, n_core, heads)
    skip = lax.all_gather(skip_gain, ("z", "core"), tiled=True)

    factor = jnp.exp(total[None, :] - within) * step
    scaled = (x * factor[..., None]).astype(bf16)
    update = jnp.einsum(
        "sgn,sghp->ghnp", b, scaled.reshape(tokens, G, per_group, width),
        preferred_element_type=f32,
    ).reshape(heads, state, width)

    own = lax.dynamic_slice_in_dim(update, c_idx * half, half, 0)
    got = swap(lax.dynamic_slice_in_dim(update, (1 - c_idx) * half, half, 0))
    first = jnp.where(c_idx == 0, own, got)
    second = jnp.where(c_idx == 0, got, own)
    mine = lax.dynamic_index_in_dim(totals, z_idx, 0, keepdims=False)
    t_first = lax.dynamic_slice_in_dim(mine[0], c_idx * half, half)
    t_second = lax.dynamic_slice_in_dim(mine[1], c_idx * half, half)
    pair = jnp.exp(t_second)[:, None, None] * first + second

    pair = pair.astype(bf16).reshape(n_z, quarter, state, width)
    rows = lax.all_to_all(pair, "z", 0, 0, tiled=True).astype(f32)
    chip_totals = lax.dynamic_slice_in_dim(
        totals[:, 0] + totals[:, 1], c_idx * half + z_idx * quarter, quarter, 1
    )
    run = jnp.zeros((quarter, state, width), f32)
    before = jnp.zeros((quarter,), f32)
    starts, lead = [], []
    for chip in range(n_z):
        starts.append(run)
        lead.append(before)
        run = jnp.exp(chip_totals[chip])[:, None, None] * run + rows[chip]
        before = before + chip_totals[chip]

    acc_t, acc_s = shift_seq((before, run), 1, n_seq)
    distance = 1
    while distance < n_seq:
        got_t, got_s = shift_seq((acc_t, acc_s), distance, n_seq)
        acc_s = jnp.exp(acc_t)[:, None, None] * got_s + acc_s
        acc_t = acc_t + got_t
        distance *= 2

    chip_in = jnp.stack(starts) + jnp.exp(jnp.stack(lead))[:, :, None, None] * acc_s[None]
    back = lax.all_to_all(chip_in.astype(bf16), "z", 0, 0, tiled=True)
    entry = back.astype(f32).reshape(half, state, width)

    into_second = jnp.exp(t_first)[:, None, None] * entry + first
    keep = jnp.where(c_idx == 0, entry, into_second).astype(bf16)
    send = jnp.where(c_idx == 0, into_second, entry).astype(bf16)
    other = swap(send)
    carried_in = jnp.where(
        c_idx == 0,
        jnp.concatenate([keep, other], axis=0),
        jnp.concatenate([other, keep], axis=0),
    )

    scores = jnp.einsum("tgn,sgn->gts", c, b, preferred_element_type=f32)
    scores = jnp.repeat(scores, per_group, axis=0)
    causal = (jnp.arange(tokens)[:, None] >= jnp.arange(tokens)[None, :])[None]
    w_t = within.T
    gap = w_t[:, :, None] - w_t[:, None, :]
    damping = jnp.where(causal, jnp.exp(jnp.where(causal, gap, 0.0)), 0.0)
    weight = (scores * damping * step.T[:, None, :]).astype(bf16)
    inside = jnp.einsum("hts,shp->thp", weight, x, preferred_element_type=f32)

    outside = jnp.einsum(
        "tgn,ghnp->tghp", c, carried_in.reshape(G, per_group, state, width),
        preferred_element_type=f32,
    ).reshape(tokens, heads, width)
    mixed = inside + jnp.exp(within)[..., None] * outside + skip[None, :, None] * x.astype(f32)
    return mixed.astype(bf16).reshape(tokens, heads * width)


def solution(mesh):
    n_seq, n_head = mesh.devices.shape
    grid = Mesh(mesh.devices.reshape(n_seq, n_head // CORES, CORES), ("seq", "z", "core"))
    rows = P(("seq", "z", "core"), None)
    in_specs = (rows, rows, rows, rows, rows, P(("z", "core")))
    return jax.shard_map(local, mesh=grid, in_specs=in_specs, out_specs=rows, check_vma=False)
```

```python
import jax
import jax.numpy as jnp
from jax import lax
from jax.sharding import Mesh
from jax.sharding import PartitionSpec as P

G = 8
CORES = 2


def swap(value):
    return lax.ppermute(value, "core", [(0, 1), (1, 0)])


def local(features, increment_per_head, token_log_decay, b_matrix, c_matrix, skip_gain):
    f32, bf16 = jnp.float32, jnp.bfloat16
    n_seq = lax.axis_size("seq")
    n_z = lax.axis_size("z")
    n_core = lax.axis_size("core")
    z_idx = lax.axis_index("z")
    c_idx = lax.axis_index("core")
    tokens = features.shape[0]
    heads = increment_per_head.shape[1]
    width = features.shape[1] // heads
    state = b_matrix.shape[1] // G
    per_group = heads // G
    half = heads // n_core
    quarter = half // n_z

    x = features.reshape(tokens, heads, width)
    step = increment_per_head.astype(f32)
    within = jnp.cumsum(token_log_decay.astype(f32), axis=0)
    total = within[-1]
    b = b_matrix.reshape(tokens, G, state)
    c = c_matrix.reshape(tokens, G, state)
    small = lax.all_gather(jnp.concatenate([total, skip_gain.astype(f32)]), ("z", "core"))
    totals = small[:, :heads].reshape(n_z, n_core, heads)
    skip = small[:, heads:].reshape(heads)

    factor = jnp.exp(total[None, :] - within) * step
    scaled = (x * factor[..., None]).astype(bf16)
    update = jnp.einsum(
        "sgn,sghp->ghnp", b, scaled.reshape(tokens, G, per_group, width),
        preferred_element_type=f32,
    ).reshape(heads, state, width)

    own = lax.dynamic_slice_in_dim(update, c_idx * half, half, 0)
    got = swap(lax.dynamic_slice_in_dim(update, (1 - c_idx) * half, half, 0))
    first = jnp.where(c_idx == 0, own, got)
    second = jnp.where(c_idx == 0, got, own)
    mine = lax.dynamic_index_in_dim(totals, z_idx, 0, keepdims=False)
    t_first = lax.dynamic_slice_in_dim(mine[0], c_idx * half, half)
    t_second = lax.dynamic_slice_in_dim(mine[1], c_idx * half, half)
    pair = jnp.exp(t_second)[:, None, None] * first + second

    pair = pair.astype(bf16).reshape(n_z, quarter, state, width)
    rows = lax.all_to_all(pair, "z", 0, 0, tiled=True).astype(f32)
    chip_totals = lax.dynamic_slice_in_dim(
        totals[:, 0] + totals[:, 1], c_idx * half + z_idx * quarter, quarter, 1
    )
    run = jnp.zeros((quarter, state, width), f32)
    before = jnp.zeros((quarter,), f32)
    starts, lead = [], []
    for chip in range(n_z):
        starts.append(run)
        lead.append(before)
        run = jnp.exp(chip_totals[chip])[:, None, None] * run + rows[chip]
        before = before + chip_totals[chip]

    piece = state // n_seq
    packed = jnp.concatenate(
        [
            run.reshape(quarter, n_seq, piece, width),
            jnp.broadcast_to(before[:, None, None, None], (quarter, n_seq, 1, width)),
        ],
        axis=2,
    ).transpose(1, 0, 2, 3)
    gathered = lax.all_to_all(packed, "seq", 0, 0, tiled=True)
    row_state = gathered[:, :, :piece]
    row_total = gathered[:, :, piece, 0]
    order = jnp.arange(n_seq)
    between = (order[None, None, :] > order[None, :, None]) & (order[None, None, :] < order[:, None, None])
    exponent = jnp.einsum(
        "abi,ih->hab", between.astype(f32), row_total, precision=lax.Precision.HIGHEST
    )
    earlier = (order[None, :] < order[:, None])[None]
    decay = jnp.where(earlier, jnp.exp(jnp.where(earlier, exponent, 0.0)), 0.0)
    entering = jnp.einsum(
        "hab,bhrw->ahrw", decay, row_state, precision=lax.Precision.HIGHEST
    )
    acc_s = lax.all_to_all(entering, "seq", 0, 0, tiled=True)
    acc_s = acc_s.transpose(1, 0, 2, 3).reshape(quarter, state, width)

    chip_in = jnp.stack(starts) + jnp.exp(jnp.stack(lead))[:, :, None, None] * acc_s[None]
    back = lax.all_to_all(chip_in.astype(bf16), "z", 0, 0, tiled=True)
    entry = back.astype(f32).reshape(half, state, width)

    into_second = jnp.exp(t_first)[:, None, None] * entry + first
    keep = jnp.where(c_idx == 0, entry, into_second).astype(bf16)
    send = jnp.where(c_idx == 0, into_second, entry).astype(bf16)
    other = swap(send)
    carried_in = jnp.where(
        c_idx == 0,
        jnp.concatenate([keep, other], axis=0),
        jnp.concatenate([other, keep], axis=0),
    )

    scores = jnp.einsum("tgn,sgn->gts", c, b, preferred_element_type=f32)
    scores = jnp.repeat(scores, per_group, axis=0)
    causal = (jnp.arange(tokens)[:, None] >= jnp.arange(tokens)[None, :])[None]
    w_t = within.T
    gap = w_t[:, :, None] - w_t[:, None, :]
    damping = jnp.where(causal, jnp.exp(jnp.where(causal, gap, 0.0)), 0.0)
    weight = (scores * damping * step.T[:, None, :]).astype(bf16)
    inside = jnp.einsum("hts,shp->thp", weight, x, preferred_element_type=f32)

    outside = jnp.einsum(
        "tgn,ghnp->tghp", c, carried_in.reshape(G, per_group, state, width),
        preferred_element_type=f32,
    ).reshape(tokens, heads, width)
    mixed = inside + jnp.exp(within)[..., None] * outside + skip[None, :, None] * x.astype(f32)
    return mixed.astype(bf16).reshape(tokens, heads * width)


def solution(mesh):
    n_seq, n_head = mesh.devices.shape
    grid = Mesh(mesh.devices.reshape(n_seq, n_head // CORES, CORES), ("seq", "z", "core"))
    rows = P(("seq", "z", "core"), None)
    in_specs = (rows, rows, rows, rows, rows, P(("z", "core")))
    return jax.shard_map(local, mesh=grid, in_specs=in_specs, out_specs=rows, check_vma=False)
```

```python
import jax
import jax.numpy as jnp
from jax import lax
from jax.sharding import Mesh
from jax.sharding import PartitionSpec as P

G = 8
CORES = 2


def swap(value):
    return lax.ppermute(value, "core", [(0, 1), (1, 0)])


def split3(value):
    hi = lax.reduce_precision(value, exponent_bits=8, mantissa_bits=7)
    rest = value - hi
    mid = lax.reduce_precision(rest, exponent_bits=8, mantissa_bits=7)
    return jnp.stack([hi, mid, rest - mid], axis=-1).astype(jnp.bfloat16)


def join3(parts):
    parts = parts.astype(jnp.float32)
    return (parts[..., 0] + parts[..., 1]) + parts[..., 2]


def lower_mask(outs, ins):
    return (jnp.arange(ins)[None, :] < jnp.arange(outs)[:, None]).astype(jnp.float32)


def decay_matrix(totals, outs):
    count = totals.shape[0]
    a = jnp.arange(outs)[:, None, None]
    b = jnp.arange(count)[None, :, None]
    m = jnp.arange(count)[None, None, :]
    between = ((b < m) & (m < a)).astype(jnp.float32)
    exponent = jnp.einsum("abm,mh->hab", between, totals, precision=lax.Precision.HIGHEST)
    earlier = (b < a)[None, :, :, 0]
    return jnp.where(earlier, jnp.exp(jnp.where(earlier, exponent, 0.0)), 0.0)


def local(features, increment_per_head, token_log_decay, b_matrix, c_matrix, skip_gain):
    f32, bf16 = jnp.float32, jnp.bfloat16
    n_seq = lax.axis_size("seq")
    n_z = lax.axis_size("z")
    n_core = lax.axis_size("core")
    z_idx = lax.axis_index("z")
    c_idx = lax.axis_index("core")
    tokens = features.shape[0]
    heads = increment_per_head.shape[1]
    width = features.shape[1] // heads
    state = b_matrix.shape[1] // G
    per_group = heads // G
    half = heads // n_core
    quarter = half // n_z

    x = features.reshape(tokens, heads, width)
    step = increment_per_head.astype(f32)
    within = jnp.cumsum(token_log_decay.astype(f32), axis=0)
    total = within[-1]
    b = b_matrix.reshape(tokens, G, state)
    c = c_matrix.reshape(tokens, G, state)
    partner = swap(jnp.concatenate([total, skip_gain.astype(f32)]))
    t_first = jnp.where(c_idx == 0, total, partner[:heads])
    t_second = jnp.where(c_idx == 0, partner[:heads], total)
    chip_skip = jnp.where(
        c_idx == 0,
        jnp.concatenate([skip_gain.astype(f32), partner[heads:]]),
        jnp.concatenate([partner[heads:], skip_gain.astype(f32)]),
    )

    factor = jnp.exp(total[None, :] - within) * step
    scaled = (x * factor[..., None]).astype(bf16)
    update = jnp.einsum(
        "sgn,sghp->ghnp", b, scaled.reshape(tokens, G, per_group, width),
        preferred_element_type=f32,
    ).reshape(heads, state, width)

    own = lax.dynamic_slice_in_dim(update, c_idx * half, half, 0)
    got = swap(lax.dynamic_slice_in_dim(update, (1 - c_idx) * half, half, 0))
    first = jnp.where(c_idx == 0, own, got)
    second = jnp.where(c_idx == 0, got, own)
    t_first = lax.dynamic_slice_in_dim(t_first, c_idx * half, half)
    t_second = lax.dynamic_slice_in_dim(t_second, c_idx * half, half)
    pair = jnp.exp(t_second)[:, None, None] * first + second

    pair = pair.astype(bf16).reshape(n_z, quarter, state, width)
    per_chip = chip_skip.shape[0]
    extra = jnp.concatenate(
        [
            split3((t_first + t_second).reshape(n_z, quarter)),
            jnp.broadcast_to(
                split3(chip_skip.reshape(quarter, per_chip // quarter)).reshape(1, quarter, -1),
                (n_z, quarter, 3 * per_chip // quarter),
            ),
        ],
        axis=-1,
    )
    extra = jnp.pad(extra, ((0, 0), (0, 0), (0, width - extra.shape[-1])))
    message = jnp.concatenate([pair, extra[:, :, None, :]], axis=2)
    rows = lax.all_to_all(message, "z", 0, 0, tiled=True)
    chip_totals = join3(rows[:, :, state, 0:3])
    skip = join3(
        rows[:, :, state, 3 : 3 + 3 * per_chip // quarter].reshape(n_z, quarter, -1, 3)
    ).reshape(heads)
    scan = jnp.einsum(
        "hab,bhnp->ahnp",
        decay_matrix(chip_totals, n_z + 1),
        rows[:, :, :state].astype(f32),
        precision=lax.Precision.HIGHEST,
    )
    leads = jnp.einsum(
        "am,mh->ah", lower_mask(n_z + 1, n_z), chip_totals, precision=lax.Precision.HIGHEST
    )
    starts, run = scan[:n_z], scan[n_z]
    lead, before = leads[:n_z], leads[n_z]

    piece = state // n_seq
    packed = jnp.concatenate(
        [
            run.reshape(quarter, n_seq, piece, width),
            jnp.broadcast_to(before[:, None, None, None], (quarter, n_seq, 1, width)),
        ],
        axis=2,
    ).transpose(1, 0, 2, 3)
    gathered = lax.all_to_all(packed, "seq", 0, 0, tiled=True)
    row_state = gathered[:, :, :piece]
    row_total = gathered[:, :, piece, 0]
    entering = jnp.einsum(
        "hab,bhrw->ahrw", decay_matrix(row_total, n_seq), row_state,
        precision=lax.Precision.HIGHEST,
    )
    acc_s = lax.all_to_all(entering, "seq", 0, 0, tiled=True)
    acc_s = acc_s.transpose(1, 0, 2, 3).reshape(quarter, state, width)

    chip_in = starts + jnp.exp(lead)[:, :, None, None] * acc_s[None]
    back = lax.all_to_all(chip_in.astype(bf16), "z", 0, 0, tiled=True)
    entry = back.astype(f32).reshape(half, state, width)

    into_second = jnp.exp(t_first)[:, None, None] * entry + first
    keep = jnp.where(c_idx == 0, entry, into_second).astype(bf16)
    send = jnp.where(c_idx == 0, into_second, entry).astype(bf16)
    other = swap(send)
    carried_in = jnp.where(
        c_idx == 0,
        jnp.concatenate([keep, other], axis=0),
        jnp.concatenate([other, keep], axis=0),
    )

    scores = jnp.einsum("tgn,sgn->gts", c, b, preferred_element_type=f32)
    scores = jnp.repeat(scores, per_group, axis=0)
    causal = (jnp.arange(tokens)[:, None] >= jnp.arange(tokens)[None, :])[None]
    w_t = within.T
    gap = w_t[:, :, None] - w_t[:, None, :]
    damping = jnp.where(causal, jnp.exp(jnp.where(causal, gap, 0.0)), 0.0)
    weight = (scores * damping * step.T[:, None, :]).astype(bf16)
    inside = jnp.einsum("hts,shp->thp", weight, x, preferred_element_type=f32)

    outside = jnp.einsum(
        "tgn,ghnp->tghp", c, carried_in.reshape(G, per_group, state, width),
        preferred_element_type=f32,
    ).reshape(tokens, heads, width)
    mixed = inside + jnp.exp(within)[..., None] * outside + skip[None, :, None] * x.astype(f32)
    return mixed.astype(bf16).reshape(tokens, heads * width)


def solution(mesh):
    n_seq, n_head = mesh.devices.shape
    grid = Mesh(mesh.devices.reshape(n_seq, n_head // CORES, CORES), ("seq", "z", "core"))
    rows = P(("seq", "z", "core"), None)
    in_specs = (rows, rows, rows, rows, rows, P(("z", "core")))
    return jax.shard_map(local, mesh=grid, in_specs=in_specs, out_specs=rows, check_vma=False)
```

```python
import jax
import jax.numpy as jnp
from jax import lax
from jax.sharding import Mesh
from jax.sharding import PartitionSpec as P

G = 8
CORES = 2


def swap(value):
    return lax.ppermute(value, "core", [(0, 1), (1, 0)])


def split3(value):
    hi = lax.reduce_precision(value, exponent_bits=8, mantissa_bits=7)
    rest = value - hi
    mid = lax.reduce_precision(rest, exponent_bits=8, mantissa_bits=7)
    return jnp.stack([hi, mid, rest - mid], axis=-1).astype(jnp.bfloat16)


def join3(parts):
    parts = parts.astype(jnp.float32)
    return (parts[..., 0] + parts[..., 1]) + parts[..., 2]


def lower_mask(outs, ins):
    return (jnp.arange(ins)[None, :] < jnp.arange(outs)[:, None]).astype(jnp.float32)


def decay_matrix(totals, outs):
    count = totals.shape[0]
    a = jnp.arange(outs)[:, None, None]
    b = jnp.arange(count)[None, :, None]
    m = jnp.arange(count)[None, None, :]
    between = ((b < m) & (m < a)).astype(jnp.float32)
    exponent = jnp.einsum("abm,mh->hab", between, totals, precision=lax.Precision.HIGHEST)
    earlier = (b < a)[None, :, :, 0]
    return jnp.where(earlier, jnp.exp(jnp.where(earlier, exponent, 0.0)), 0.0)


def local(features, increment_per_head, token_log_decay, b_matrix, c_matrix, skip_gain):
    f32, bf16 = jnp.float32, jnp.bfloat16
    n_seq = lax.axis_size("seq")
    n_z = lax.axis_size("z")
    n_core = lax.axis_size("core")
    z_idx = lax.axis_index("z")
    c_idx = lax.axis_index("core")
    tokens = features.shape[0]
    heads = increment_per_head.shape[1]
    width = features.shape[1] // heads
    state = b_matrix.shape[1] // G
    per_group = heads // G
    half = heads // n_core
    quarter = half // n_z

    x = features.reshape(tokens, heads, width)
    step = increment_per_head.astype(f32)
    within = jnp.cumsum(token_log_decay.astype(f32), axis=0)
    total = within[-1]
    b = b_matrix.reshape(tokens, G, state)
    c = c_matrix.reshape(tokens, G, state)
    partner = swap(jnp.concatenate([total, skip_gain.astype(f32)]))
    t_first = jnp.where(c_idx == 0, total, partner[:heads])
    t_second = jnp.where(c_idx == 0, partner[:heads], total)
    chip_skip = jnp.where(
        c_idx == 0,
        jnp.concatenate([skip_gain.astype(f32), partner[heads:]]),
        jnp.concatenate([partner[heads:], skip_gain.astype(f32)]),
    )

    factor = jnp.exp(total[None, :] - within) * step
    scaled = (x * factor[..., None]).astype(bf16)
    update = jnp.einsum(
        "sgn,sghp->ghnp", b, scaled.reshape(tokens, G, per_group, width),
        preferred_element_type=f32,
    ).reshape(heads, state, width)

    own = lax.dynamic_slice_in_dim(update, c_idx * half, half, 0)
    got = swap(lax.dynamic_slice_in_dim(update, (1 - c_idx) * half, half, 0))
    first = jnp.where(c_idx == 0, own, got)
    second = jnp.where(c_idx == 0, got, own)
    t_first = lax.dynamic_slice_in_dim(t_first, c_idx * half, half)
    t_second = lax.dynamic_slice_in_dim(t_second, c_idx * half, half)
    pair = jnp.exp(t_second)[:, None, None] * first + second

    pair = pair.astype(bf16).reshape(n_z, quarter, state, width)
    per_chip = chip_skip.shape[0]
    extra = jnp.concatenate(
        [
            split3((t_first + t_second).reshape(n_z, quarter)),
            jnp.broadcast_to(
                split3(chip_skip.reshape(quarter, per_chip // quarter)).reshape(1, quarter, -1),
                (n_z, quarter, 3 * per_chip // quarter),
            ),
        ],
        axis=-1,
    )
    extra = jnp.pad(extra, ((0, 0), (0, 0), (0, width - extra.shape[-1])))
    message = jnp.concatenate([pair, extra[:, :, None, :]], axis=2)
    rows = lax.all_to_all(message, "z", 0, 0, tiled=True)
    scores = jnp.einsum("tgn,sgn->gts", c, b, preferred_element_type=f32)
    scores = jnp.repeat(scores, per_group, axis=0)
    causal = (jnp.arange(tokens)[:, None] >= jnp.arange(tokens)[None, :])[None]
    w_t = within.T
    gap = w_t[:, :, None] - w_t[:, None, :]
    damping = jnp.where(causal, jnp.exp(jnp.where(causal, gap, 0.0)), 0.0)
    weight = (scores * damping * step.T[:, None, :]).astype(bf16)
    inside = jnp.einsum("hts,shp->thp", weight, x, preferred_element_type=f32)

    inside, rows = lax.optimization_barrier((inside, rows))
    chip_totals = join3(rows[:, :, state, 0:3])
    skip = join3(
        rows[:, :, state, 3 : 3 + 3 * per_chip // quarter].reshape(n_z, quarter, -1, 3)
    ).reshape(heads)
    scan = jnp.einsum(
        "hab,bhnp->ahnp",
        decay_matrix(chip_totals, n_z + 1),
        rows[:, :, :state].astype(f32),
        precision=lax.Precision.HIGHEST,
    )
    leads = jnp.einsum(
        "am,mh->ah", lower_mask(n_z + 1, n_z), chip_totals, precision=lax.Precision.HIGHEST
    )
    starts, run = scan[:n_z], scan[n_z]
    lead, before = leads[:n_z], leads[n_z]

    piece = state // n_seq
    packed = jnp.concatenate(
        [
            run.reshape(quarter, n_seq, piece, width),
            jnp.broadcast_to(before[:, None, None, None], (quarter, n_seq, 1, width)),
        ],
        axis=2,
    ).transpose(1, 0, 2, 3)
    gathered = lax.all_to_all(packed, "seq", 0, 0, tiled=True)
    row_state = gathered[:, :, :piece]
    row_total = gathered[:, :, piece, 0]
    entering = jnp.einsum(
        "hab,bhrw->ahrw", decay_matrix(row_total, n_seq), row_state,
        precision=lax.Precision.HIGHEST,
    )
    acc_s = lax.all_to_all(entering, "seq", 0, 0, tiled=True)
    acc_s = acc_s.transpose(1, 0, 2, 3).reshape(quarter, state, width)

    chip_in = starts + jnp.exp(lead)[:, :, None, None] * acc_s[None]
    back = lax.all_to_all(chip_in.astype(bf16), "z", 0, 0, tiled=True)
    entry = back.astype(f32).reshape(half, state, width)

    into_second = jnp.exp(t_first)[:, None, None] * entry + first
    keep = jnp.where(c_idx == 0, entry, into_second).astype(bf16)
    send = jnp.where(c_idx == 0, into_second, entry).astype(bf16)
    other = swap(send)
    carried_in = jnp.where(
        c_idx == 0,
        jnp.concatenate([keep, other], axis=0),
        jnp.concatenate([other, keep], axis=0),
    )

    outside = jnp.einsum(
        "tgn,ghnp->tghp", c, carried_in.reshape(G, per_group, state, width),
        preferred_element_type=f32,
    ).reshape(tokens, heads, width)
    mixed = inside + jnp.exp(within)[..., None] * outside + skip[None, :, None] * x.astype(f32)
    return mixed.astype(bf16).reshape(tokens, heads * width)


def solution(mesh):
    n_seq, n_head = mesh.devices.shape
    grid = Mesh(mesh.devices.reshape(n_seq, n_head // CORES, CORES), ("seq", "z", "core"))
    rows = P(("seq", "z", "core"), None)
    in_specs = (rows, rows, rows, rows, rows, P(("z", "core")))
    return jax.shard_map(local, mesh=grid, in_specs=in_specs, out_specs=rows, check_vma=False)
```

```python
import jax
import jax.numpy as jnp
from jax import lax
from jax.sharding import Mesh
from jax.sharding import PartitionSpec as P

G = 8
CORES = 2


def swap(value):
    return lax.ppermute(value, "core", [(0, 1), (1, 0)])


def split3(value):
    hi = lax.reduce_precision(value, exponent_bits=8, mantissa_bits=7)
    rest = value - hi
    mid = lax.reduce_precision(rest, exponent_bits=8, mantissa_bits=7)
    return jnp.stack([hi, mid, rest - mid], axis=-1).astype(jnp.bfloat16)


def join3(parts):
    parts = parts.astype(jnp.float32)
    return (parts[..., 0] + parts[..., 1]) + parts[..., 2]


def lower_mask(outs, ins):
    return (jnp.arange(ins)[None, :] < jnp.arange(outs)[:, None]).astype(jnp.float32)


def decay_matrix(totals, outs):
    count = totals.shape[0]
    a = jnp.arange(outs)[:, None, None]
    b = jnp.arange(count)[None, :, None]
    m = jnp.arange(count)[None, None, :]
    between = ((b < m) & (m < a)).astype(jnp.float32)
    exponent = jnp.einsum("abm,mh->hab", between, totals, precision=lax.Precision.HIGHEST)
    earlier = (b < a)[None, :, :, 0]
    return jnp.where(earlier, jnp.exp(jnp.where(earlier, exponent, 0.0)), 0.0)


def local(features, increment_per_head, token_log_decay, b_matrix, c_matrix, skip_gain):
    f32, bf16 = jnp.float32, jnp.bfloat16
    n_seq = lax.axis_size("seq")
    n_z = lax.axis_size("z")
    n_core = lax.axis_size("core")
    z_idx = lax.axis_index("z")
    c_idx = lax.axis_index("core")
    tokens = features.shape[0]
    heads = increment_per_head.shape[1]
    width = features.shape[1] // heads
    state = b_matrix.shape[1] // G
    per_group = heads // G
    half = heads // n_core
    quarter = half // n_z

    x = features.reshape(tokens, heads, width)
    step = increment_per_head.astype(f32)
    within = jnp.cumsum(token_log_decay.astype(f32), axis=0)
    total = within[-1]
    b = b_matrix.reshape(tokens, G, state)
    c = c_matrix.reshape(tokens, G, state)
    partner = swap(jnp.concatenate([total, skip_gain.astype(f32)]))
    t_first = jnp.where(c_idx == 0, total, partner[:heads])
    t_second = jnp.where(c_idx == 0, partner[:heads], total)
    chip_skip = jnp.where(
        c_idx == 0,
        jnp.concatenate([skip_gain.astype(f32), partner[heads:]]),
        jnp.concatenate([partner[heads:], skip_gain.astype(f32)]),
    )

    factor = jnp.exp(total[None, :] - within) * step
    scaled = (x * factor[..., None]).astype(bf16)
    update = jnp.einsum(
        "sgn,sghp->ghnp", b, scaled.reshape(tokens, G, per_group, width),
        preferred_element_type=f32,
    ).reshape(heads, state, width)

    own = lax.dynamic_slice_in_dim(update, c_idx * half, half, 0)
    got = swap(lax.dynamic_slice_in_dim(update, (1 - c_idx) * half, half, 0))
    first = jnp.where(c_idx == 0, own, got)
    second = jnp.where(c_idx == 0, got, own)
    t_first = lax.dynamic_slice_in_dim(t_first, c_idx * half, half)
    t_second = lax.dynamic_slice_in_dim(t_second, c_idx * half, half)
    pair = jnp.exp(t_second)[:, None, None] * first + second

    pair = pair.astype(bf16).reshape(n_z, quarter, state, width)
    per_chip = chip_skip.shape[0]
    extra = jnp.concatenate(
        [
            split3((t_first + t_second).reshape(n_z, quarter)),
            jnp.broadcast_to(
                split3(chip_skip.reshape(quarter, per_chip // quarter)).reshape(1, quarter, -1),
                (n_z, quarter, 3 * per_chip // quarter),
            ),
        ],
        axis=-1,
    )
    extra = jnp.pad(extra, ((0, 0), (0, 0), (0, width - extra.shape[-1])))
    message = jnp.concatenate([pair, extra[:, :, None, :]], axis=2)
    rows = lax.all_to_all(message, "z", 0, 0, tiled=True)
    scores = jnp.einsum("tgn,sgn->gts", c, b, preferred_element_type=f32)
    scores = jnp.repeat(scores, per_group, axis=0)
    causal = (jnp.arange(tokens)[:, None] >= jnp.arange(tokens)[None, :])[None]
    w_t = within.T
    gap = w_t[:, :, None] - w_t[:, None, :]
    damping = jnp.where(causal, jnp.exp(jnp.where(causal, gap, 0.0)), 0.0)
    weight = (scores * damping * step.T[:, None, :]).astype(bf16)
    inside = jnp.einsum("hts,shp->thp", weight, x, preferred_element_type=f32)

    chip_totals = join3(rows[:, :, state, 0:3])
    inside, chip_totals = lax.optimization_barrier((inside, chip_totals))
    skip = join3(
        rows[:, :, state, 3 : 3 + 3 * per_chip // quarter].reshape(n_z, quarter, -1, 3)
    ).reshape(heads)
    scan = jnp.einsum(
        "hab,bhnp->ahnp",
        decay_matrix(chip_totals, n_z + 1),
        rows[:, :, :state].astype(f32),
        precision=lax.Precision.HIGHEST,
    )
    leads = jnp.einsum(
        "am,mh->ah", lower_mask(n_z + 1, n_z), chip_totals, precision=lax.Precision.HIGHEST
    )
    starts, run = scan[:n_z], scan[n_z]
    lead, before = leads[:n_z], leads[n_z]

    piece = state // n_seq
    packed = jnp.concatenate(
        [
            run.reshape(quarter, n_seq, piece, width),
            jnp.broadcast_to(before[:, None, None, None], (quarter, n_seq, 1, width)),
        ],
        axis=2,
    ).transpose(1, 0, 2, 3)
    gathered = lax.all_to_all(packed, "seq", 0, 0, tiled=True)
    row_state = gathered[:, :, :piece]
    row_total = gathered[:, :, piece, 0]
    entering = jnp.einsum(
        "hab,bhrw->ahrw", decay_matrix(row_total, n_seq), row_state,
        precision=lax.Precision.HIGHEST,
    )
    acc_s = lax.all_to_all(entering, "seq", 0, 0, tiled=True)
    acc_s = acc_s.transpose(1, 0, 2, 3).reshape(quarter, state, width)

    chip_in = starts + jnp.exp(lead)[:, :, None, None] * acc_s[None]
    back = lax.all_to_all(chip_in.astype(bf16), "z", 0, 0, tiled=True)
    entry = back.astype(f32).reshape(half, state, width)

    into_second = jnp.exp(t_first)[:, None, None] * entry + first
    keep = jnp.where(c_idx == 0, entry, into_second).astype(bf16)
    send = jnp.where(c_idx == 0, into_second, entry).astype(bf16)
    other = swap(send)
    carried_in = jnp.where(
        c_idx == 0,
        jnp.concatenate([keep, other], axis=0),
        jnp.concatenate([other, keep], axis=0),
    )

    outside = jnp.einsum(
        "tgn,ghnp->tghp", c, carried_in.reshape(G, per_group, state, width),
        preferred_element_type=f32,
    ).reshape(tokens, heads, width)
    mixed = inside + jnp.exp(within)[..., None] * outside + skip[None, :, None] * x.astype(f32)
    return mixed.astype(bf16).reshape(tokens, heads * width)


def solution(mesh):
    n_seq, n_head = mesh.devices.shape
    grid = Mesh(mesh.devices.reshape(n_seq, n_head // CORES, CORES), ("seq", "z", "core"))
    rows = P(("seq", "z", "core"), None)
    in_specs = (rows, rows, rows, rows, rows, P(("z", "core")))
    return jax.shard_map(local, mesh=grid, in_specs=in_specs, out_specs=rows, check_vma=False)
```

```python
import jax
import jax.numpy as jnp
from jax import lax
from jax.sharding import Mesh
from jax.sharding import PartitionSpec as P

G = 8
CORES = 2


def swap(value):
    return lax.ppermute(value, "core", [(0, 1), (1, 0)])


def split3(value):
    hi = lax.reduce_precision(value, exponent_bits=8, mantissa_bits=7)
    rest = value - hi
    mid = lax.reduce_precision(rest, exponent_bits=8, mantissa_bits=7)
    return jnp.stack([hi, mid, rest - mid], axis=-1).astype(jnp.bfloat16)


def join3(parts):
    parts = parts.astype(jnp.float32)
    return (parts[..., 0] + parts[..., 1]) + parts[..., 2]


def lower_mask(outs, ins):
    return (jnp.arange(ins)[None, :] < jnp.arange(outs)[:, None]).astype(jnp.float32)


def decay_matrix(totals, outs):
    count = totals.shape[0]
    a = jnp.arange(outs)[:, None, None]
    b = jnp.arange(count)[None, :, None]
    m = jnp.arange(count)[None, None, :]
    between = ((b < m) & (m < a)).astype(jnp.float32)
    exponent = jnp.einsum("abm,mh->hab", between, totals, precision=lax.Precision.HIGHEST)
    earlier = (b < a)[None, :, :, 0]
    return jnp.where(earlier, jnp.exp(jnp.where(earlier, exponent, 0.0)), 0.0)


def local(features, increment_per_head, token_log_decay, b_matrix, c_matrix, skip_gain):
    f32, bf16 = jnp.float32, jnp.bfloat16
    n_seq = lax.axis_size("seq")
    n_z = lax.axis_size("z")
    n_core = lax.axis_size("core")
    z_idx = lax.axis_index("z")
    c_idx = lax.axis_index("core")
    tokens = features.shape[0]
    heads = increment_per_head.shape[1]
    width = features.shape[1] // heads
    state = b_matrix.shape[1] // G
    per_group = heads // G
    half = heads // n_core
    quarter = half // n_z

    x = features.reshape(tokens, heads, width)
    step = increment_per_head.astype(f32)
    within = jnp.cumsum(token_log_decay.astype(f32), axis=0)
    total = within[-1]
    b = b_matrix.reshape(tokens, G, state)
    c = c_matrix.reshape(tokens, G, state)
    partner = swap(jnp.concatenate([total, skip_gain.astype(f32)]))
    t_first = jnp.where(c_idx == 0, total, partner[:heads])
    t_second = jnp.where(c_idx == 0, partner[:heads], total)
    chip_skip = jnp.where(
        c_idx == 0,
        jnp.concatenate([skip_gain.astype(f32), partner[heads:]]),
        jnp.concatenate([partner[heads:], skip_gain.astype(f32)]),
    )

    factor = jnp.exp(total[None, :] - within) * step
    scaled = (x * factor[..., None]).astype(bf16)
    update = jnp.einsum(
        "sgn,sgk->gnk", b, scaled.reshape(tokens, G, per_group * width),
        preferred_element_type=f32,
    )

    groups = G // n_core
    own = lax.dynamic_slice_in_dim(update, c_idx * groups, groups, 0)
    got = swap(lax.dynamic_slice_in_dim(update, (1 - c_idx) * groups, groups, 0))
    first = jnp.where(c_idx == 0, own, got)
    second = jnp.where(c_idx == 0, got, own)
    t_first = lax.dynamic_slice_in_dim(t_first, c_idx * half, half)
    t_second = lax.dynamic_slice_in_dim(t_second, c_idx * half, half)
    def spread(v):
        return jnp.repeat(v.reshape(groups, 1, per_group), width, axis=2)

    pair = spread(jnp.exp(t_second)) * first + second

    split = per_group // quarter
    pair = (
        pair.astype(bf16)
        .reshape(groups, state, split, quarter, width)
        .transpose(0, 2, 3, 1, 4)
        .reshape(n_z, quarter, state, width)
    )
    per_chip = chip_skip.shape[0]
    extra = jnp.concatenate(
        [
            split3((t_first + t_second).reshape(n_z, quarter)),
            jnp.broadcast_to(
                split3(chip_skip.reshape(quarter, per_chip // quarter)).reshape(1, quarter, -1),
                (n_z, quarter, 3 * per_chip // quarter),
            ),
        ],
        axis=-1,
    )
    extra = jnp.pad(extra, ((0, 0), (0, 0), (0, width - extra.shape[-1])))
    message = jnp.concatenate([pair, extra[:, :, None, :]], axis=2)
    rows = lax.all_to_all(message, "z", 0, 0, tiled=True)
    scores = jnp.einsum("tgn,sgn->gts", c, b, preferred_element_type=f32)
    scores = jnp.repeat(scores, per_group, axis=0)
    causal = (jnp.arange(tokens)[:, None] >= jnp.arange(tokens)[None, :])[None]
    w_t = within.T
    gap = w_t[:, :, None] - w_t[:, None, :]
    damping = jnp.where(causal, jnp.exp(jnp.where(causal, gap, 0.0)), 0.0)
    weight = (scores * damping * step.T[:, None, :]).astype(bf16)
    inside = jnp.einsum("hts,shp->thp", weight, x, preferred_element_type=f32)

    chip_totals = join3(rows[:, :, state, 0:3])
    inside, chip_totals = lax.optimization_barrier((inside, chip_totals))
    skip = join3(
        rows[:, :, state, 3 : 3 + 3 * per_chip // quarter].reshape(n_z, quarter, -1, 3)
    ).reshape(heads)
    scan = jnp.einsum(
        "hab,bhnp->ahnp",
        decay_matrix(chip_totals, n_z + 1),
        rows[:, :, :state].astype(f32),
        precision=lax.Precision.HIGHEST,
    )
    leads = jnp.einsum(
        "am,mh->ah", lower_mask(n_z + 1, n_z), chip_totals, precision=lax.Precision.HIGHEST
    )
    starts, run = scan[:n_z], scan[n_z]
    lead, before = leads[:n_z], leads[n_z]

    piece = state // n_seq
    packed = jnp.concatenate(
        [
            run.reshape(quarter, n_seq, piece, width),
            jnp.broadcast_to(before[:, None, None, None], (quarter, n_seq, 1, width)),
        ],
        axis=2,
    ).transpose(1, 0, 2, 3)
    gathered = lax.all_to_all(packed, "seq", 0, 0, tiled=True)
    row_state = gathered[:, :, :piece]
    row_total = gathered[:, :, piece, 0]
    entering = jnp.einsum(
        "hab,bhrw->ahrw", decay_matrix(row_total, n_seq), row_state,
        precision=lax.Precision.HIGHEST,
    )
    acc_s = lax.all_to_all(entering, "seq", 0, 0, tiled=True)
    acc_s = acc_s.transpose(1, 0, 2, 3).reshape(quarter, state, width)

    chip_in = starts + jnp.exp(lead)[:, :, None, None] * acc_s[None]
    back = lax.all_to_all(chip_in.astype(bf16), "z", 0, 0, tiled=True)
    entry = (
        back.astype(f32)
        .reshape(groups, split, quarter, state, width)
        .transpose(0, 3, 1, 2, 4)
        .reshape(groups, state, per_group * width)
    )

    into_second = spread(jnp.exp(t_first)) * entry + first
    keep = jnp.where(c_idx == 0, entry, into_second).astype(bf16)
    send = jnp.where(c_idx == 0, into_second, entry).astype(bf16)
    other = swap(send)
    carried_in = jnp.where(
        c_idx == 0,
        jnp.concatenate([keep, other], axis=0),
        jnp.concatenate([other, keep], axis=0),
    )

    outside = jnp.einsum(
        "tgn,gnk->tgk", c, carried_in, preferred_element_type=f32
    ).reshape(tokens, heads, width)
    mixed = inside + jnp.exp(within)[..., None] * outside + skip[None, :, None] * x.astype(f32)
    return mixed.astype(bf16).reshape(tokens, heads * width)


def solution(mesh):
    n_seq, n_head = mesh.devices.shape
    grid = Mesh(mesh.devices.reshape(n_seq, n_head // CORES, CORES), ("seq", "z", "core"))
    rows = P(("seq", "z", "core"), None)
    in_specs = (rows, rows, rows, rows, rows, P(("z", "core")))
    return jax.shard_map(local, mesh=grid, in_specs=in_specs, out_specs=rows, check_vma=False)
```

```python
import jax
import jax.numpy as jnp
from jax import lax
from jax.sharding import Mesh
from jax.sharding import PartitionSpec as P

G = 8
CORES = 2


def swap(value):
    return lax.ppermute(value, "core", [(0, 1), (1, 0)])


def split3(value):
    hi = lax.reduce_precision(value, exponent_bits=8, mantissa_bits=7)
    rest = value - hi
    mid = lax.reduce_precision(rest, exponent_bits=8, mantissa_bits=7)
    return jnp.stack([hi, mid, rest - mid], axis=-1).astype(jnp.bfloat16)


def join3(parts):
    parts = parts.astype(jnp.float32)
    return (parts[..., 0] + parts[..., 1]) + parts[..., 2]


def lower_mask(outs, ins):
    return (jnp.arange(ins)[None, :] < jnp.arange(outs)[:, None]).astype(jnp.float32)


def decay_matrix(totals, outs):
    count = totals.shape[0]
    a = jnp.arange(outs)[:, None, None]
    b = jnp.arange(count)[None, :, None]
    m = jnp.arange(count)[None, None, :]
    between = ((b < m) & (m < a)).astype(jnp.float32)
    exponent = jnp.einsum("abm,mh->hab", between, totals, precision=lax.Precision.HIGHEST)
    earlier = (b < a)[None, :, :, 0]
    return jnp.where(earlier, jnp.exp(jnp.where(earlier, exponent, 0.0)), 0.0)


def local(features, increment_per_head, token_log_decay, b_matrix, c_matrix, skip_gain):
    f32, bf16 = jnp.float32, jnp.bfloat16
    n_seq = lax.axis_size("seq")
    n_z = lax.axis_size("z")
    n_core = lax.axis_size("core")
    z_idx = lax.axis_index("z")
    c_idx = lax.axis_index("core")
    tokens = features.shape[0]
    heads = increment_per_head.shape[1]
    width = features.shape[1] // heads
    state = b_matrix.shape[1] // G
    per_group = heads // G
    half = heads // n_core
    quarter = half // n_z

    x = features.reshape(tokens, heads, width)
    step = increment_per_head.astype(f32)
    within = jnp.cumsum(token_log_decay.astype(f32), axis=0)
    total = within[-1]
    b = b_matrix.reshape(tokens, G, state)
    c = c_matrix.reshape(tokens, G, state)
    partner = swap(jnp.concatenate([total, skip_gain.astype(f32)]))
    t_first = jnp.where(c_idx == 0, total, partner[:heads])
    t_second = jnp.where(c_idx == 0, partner[:heads], total)
    chip_skip = jnp.where(
        c_idx == 0,
        jnp.concatenate([skip_gain.astype(f32), partner[heads:]]),
        jnp.concatenate([partner[heads:], skip_gain.astype(f32)]),
    )

    factor = jnp.exp(total[None, :] - within) * step
    scaled = (x * factor[..., None]).astype(bf16)
    update = jnp.einsum(
        "sgn,sghp->ghnp", b, scaled.reshape(tokens, G, per_group, width),
        preferred_element_type=f32,
    ).reshape(heads, state, width)

    own = lax.dynamic_slice_in_dim(update, c_idx * half, half, 0)
    got = swap(lax.dynamic_slice_in_dim(update, (1 - c_idx) * half, half, 0))
    first = jnp.where(c_idx == 0, own, got)
    second = jnp.where(c_idx == 0, got, own)
    t_first = lax.dynamic_slice_in_dim(t_first, c_idx * half, half)
    t_second = lax.dynamic_slice_in_dim(t_second, c_idx * half, half)
    pair = jnp.exp(t_second)[:, None, None] * first + second

    pair = pair.astype(bf16).reshape(n_z, quarter, state, width)
    per_chip = chip_skip.shape[0]
    extra = jnp.concatenate(
        [
            split3((t_first + t_second).reshape(n_z, quarter)),
            jnp.broadcast_to(
                split3(chip_skip.reshape(quarter, per_chip // quarter)).reshape(1, quarter, -1),
                (n_z, quarter, 3 * per_chip // quarter),
            ),
        ],
        axis=-1,
    )
    extra = jnp.pad(
        extra, ((0, 0), (0, state - quarter), (0, width - extra.shape[-1]))
    )
    message = jnp.concatenate([pair, extra[:, None]], axis=1)
    rows = lax.all_to_all(message, "z", 0, 0, tiled=True)
    scores = jnp.einsum("tgn,sgn->gts", c, b, preferred_element_type=f32)
    scores = jnp.repeat(scores, per_group, axis=0)
    causal = (jnp.arange(tokens)[:, None] >= jnp.arange(tokens)[None, :])[None]
    w_t = within.T
    gap = w_t[:, :, None] - w_t[:, None, :]
    damping = jnp.where(causal, jnp.exp(jnp.where(causal, gap, 0.0)), 0.0)
    weight = (scores * damping * step.T[:, None, :]).astype(bf16)
    inside = jnp.einsum("hts,shp->thp", weight, x, preferred_element_type=f32)

    chip_totals = join3(rows[:, quarter, :quarter, 0:3])
    inside, chip_totals = lax.optimization_barrier((inside, chip_totals))
    skip = join3(
        rows[:, quarter, :quarter, 3 : 3 + 3 * per_chip // quarter].reshape(
            n_z, quarter, -1, 3
        )
    ).reshape(heads)
    scan = jnp.einsum(
        "hab,bhnp->ahnp",
        decay_matrix(chip_totals, n_z + 1),
        rows[:, :quarter].astype(f32),
        precision=lax.Precision.HIGHEST,
    )
    leads = jnp.einsum(
        "am,mh->ah", lower_mask(n_z + 1, n_z), chip_totals, precision=lax.Precision.HIGHEST
    )
    starts, run = scan[:n_z], scan[n_z]
    lead, before = leads[:n_z], leads[n_z]

    piece = state // n_seq
    packed = jnp.concatenate(
        [
            run.reshape(quarter, n_seq, piece, width),
            jnp.broadcast_to(before[:, None, None, None], (quarter, n_seq, 1, width)),
        ],
        axis=2,
    ).transpose(1, 0, 2, 3)
    gathered = lax.all_to_all(packed, "seq", 0, 0, tiled=True)
    row_state = gathered[:, :, :piece]
    row_total = gathered[:, :, piece, 0]
    entering = jnp.einsum(
        "hab,bhrw->ahrw", decay_matrix(row_total, n_seq), row_state,
        precision=lax.Precision.HIGHEST,
    )
    acc_s = lax.all_to_all(entering, "seq", 0, 0, tiled=True)
    acc_s = acc_s.transpose(1, 0, 2, 3).reshape(quarter, state, width)

    chip_in = starts + jnp.exp(lead)[:, :, None, None] * acc_s[None]
    back = lax.all_to_all(chip_in.astype(bf16), "z", 0, 0, tiled=True)
    entry = back.astype(f32).reshape(half, state, width)

    into_second = jnp.exp(t_first)[:, None, None] * entry + first
    keep = jnp.where(c_idx == 0, entry, into_second).astype(bf16)
    send = jnp.where(c_idx == 0, into_second, entry).astype(bf16)
    other = swap(send)
    carried_in = jnp.where(
        c_idx == 0,
        jnp.concatenate([keep, other], axis=0),
        jnp.concatenate([other, keep], axis=0),
    )

    outside = jnp.einsum(
        "tgn,ghnp->tghp", c, carried_in.reshape(G, per_group, state, width),
        preferred_element_type=f32,
    ).reshape(tokens, heads, width)
    mixed = inside + jnp.exp(within)[..., None] * outside + skip[None, :, None] * x.astype(f32)
    return mixed.astype(bf16).reshape(tokens, heads * width)


def solution(mesh):
    n_seq, n_head = mesh.devices.shape
    grid = Mesh(mesh.devices.reshape(n_seq, n_head // CORES, CORES), ("seq", "z", "core"))
    rows = P(("seq", "z", "core"), None)
    in_specs = (rows, rows, rows, rows, rows, P(("z", "core")))
    return jax.shard_map(local, mesh=grid, in_specs=in_specs, out_specs=rows, check_vma=False)
```

```python
import jax
import jax.numpy as jnp
from jax import lax
from jax.sharding import Mesh
from jax.sharding import PartitionSpec as P

G = 8
CORES = 2


def swap(value):
    return lax.ppermute(value, "core", [(0, 1), (1, 0)])


def split3(value):
    hi = lax.reduce_precision(value, exponent_bits=8, mantissa_bits=7)
    rest = value - hi
    mid = lax.reduce_precision(rest, exponent_bits=8, mantissa_bits=7)
    return jnp.stack([hi, mid, rest - mid], axis=-1).astype(jnp.bfloat16)


def join3(parts):
    parts = parts.astype(jnp.float32)
    return (parts[..., 0] + parts[..., 1]) + parts[..., 2]


def lower_mask(outs, ins):
    return (jnp.arange(ins)[None, :] < jnp.arange(outs)[:, None]).astype(jnp.float32)


def decay_matrix(totals, outs):
    count = totals.shape[0]
    a = jnp.arange(outs)[:, None, None]
    b = jnp.arange(count)[None, :, None]
    m = jnp.arange(count)[None, None, :]
    between = ((b < m) & (m < a)).astype(jnp.float32)
    exponent = jnp.einsum("abm,mh->hab", between, totals, precision=lax.Precision.HIGHEST)
    earlier = (b < a)[None, :, :, 0]
    return jnp.where(earlier, jnp.exp(jnp.where(earlier, exponent, 0.0)), 0.0)


def local(features, increment_per_head, token_log_decay, b_matrix, c_matrix, skip_gain):
    f32, bf16 = jnp.float32, jnp.bfloat16
    n_seq = lax.axis_size("seq")
    n_z = lax.axis_size("z")
    n_core = lax.axis_size("core")
    z_idx = lax.axis_index("z")
    c_idx = lax.axis_index("core")
    tokens = features.shape[0]
    heads = increment_per_head.shape[1]
    width = features.shape[1] // heads
    state = b_matrix.shape[1] // G
    per_group = heads // G
    half = heads // n_core
    quarter = half // n_z

    x = features.reshape(tokens, heads, width)
    step = increment_per_head.astype(f32)
    within = jnp.cumsum(token_log_decay.astype(f32), axis=0)
    total = within[-1]
    b = b_matrix.reshape(tokens, G, state)
    c = c_matrix.reshape(tokens, G, state)
    partner = swap(jnp.concatenate([total, skip_gain.astype(f32)]))
    t_first = jnp.where(c_idx == 0, total, partner[:heads])
    t_second = jnp.where(c_idx == 0, partner[:heads], total)
    chip_skip = jnp.where(
        c_idx == 0,
        jnp.concatenate([skip_gain.astype(f32), partner[heads:]]),
        jnp.concatenate([partner[heads:], skip_gain.astype(f32)]),
    )

    factor = jnp.exp(total[None, :] - within) * step
    scaled = (x * factor[..., None]).astype(bf16)
    update = jnp.einsum(
        "sgn,sghp->ghnp", b, scaled.reshape(tokens, G, per_group, width),
        preferred_element_type=f32,
    ).reshape(heads, state, width)

    own = lax.dynamic_slice_in_dim(update, c_idx * half, half, 0)
    got = swap(lax.dynamic_slice_in_dim(update, (1 - c_idx) * half, half, 0))
    first = jnp.where(c_idx == 0, own, got)
    second = jnp.where(c_idx == 0, got, own)
    t_first = lax.dynamic_slice_in_dim(t_first, c_idx * half, half)
    t_second = lax.dynamic_slice_in_dim(t_second, c_idx * half, half)
    pair = jnp.exp(t_second)[:, None, None] * first + second

    pair = pair.astype(bf16).reshape(n_z, quarter, state, width)
    per_chip = chip_skip.shape[0]
    extra = jnp.concatenate(
        [
            split3((t_first + t_second).reshape(n_z, quarter)),
            jnp.broadcast_to(
                split3(chip_skip.reshape(quarter, per_chip // quarter)).reshape(1, quarter, -1),
                (n_z, quarter, 3 * per_chip // quarter),
            ),
        ],
        axis=-1,
    )
    extra = jnp.pad(
        extra, ((0, 0), (0, state - quarter), (0, width - extra.shape[-1]))
    )
    message = jnp.concatenate([pair, extra[:, None]], axis=1)
    rows = lax.all_to_all(message, "z", 0, 0, tiled=True)
    scores = jnp.einsum("tgn,sgn->gts", c, b, preferred_element_type=f32)
    scores = jnp.repeat(scores, per_group, axis=0)
    causal = (jnp.arange(tokens)[:, None] >= jnp.arange(tokens)[None, :])[None]
    w_t = within.T
    gap = w_t[:, :, None] - w_t[:, None, :]
    damping = jnp.where(causal, jnp.exp(jnp.where(causal, gap, 0.0)), 0.0)
    weight = (scores * damping * step.T[:, None, :]).astype(bf16)
    inside = jnp.einsum("hts,shp->thp", weight, x, preferred_element_type=f32)

    chip_totals = join3(rows[:, quarter, :quarter, 0:3])
    inside, chip_totals = lax.optimization_barrier((inside, chip_totals))
    skip = join3(
        rows[:, quarter, :quarter, 3 : 3 + 3 * per_chip // quarter].reshape(
            n_z, quarter, -1, 3
        )
    ).reshape(heads)
    scan = jnp.einsum(
        "hab,bhnp->ahnp",
        decay_matrix(chip_totals, n_z + 1),
        rows[:, :quarter].astype(f32),
        precision=lax.Precision.HIGHEST,
    )
    leads = jnp.einsum(
        "am,mh->ah", lower_mask(n_z + 1, n_z), chip_totals, precision=lax.Precision.HIGHEST
    )
    starts, run = scan[:n_z], scan[n_z]
    lead, before = leads[:n_z], leads[n_z]

    per = quarter * width // n_seq
    chunks = run.transpose(0, 2, 1).reshape(n_seq, per, state)
    row_totals = jnp.repeat(before, width).reshape(n_seq, per)
    packed = jnp.concatenate(
        [chunks, jnp.pad(row_totals, ((0, 0), (0, state - per)))[:, None, :]], axis=1
    )
    gathered = lax.all_to_all(packed, "seq", 0, 0, tiled=True)
    entering = jnp.einsum(
        "rab,brn->arn",
        decay_matrix(gathered[:, per, :per], n_seq),
        gathered[:, :per],
        precision=lax.Precision.HIGHEST,
    )
    acc_s = lax.all_to_all(entering, "seq", 0, 0, tiled=True)
    acc_s = acc_s.reshape(quarter, width, state).transpose(0, 2, 1)

    chip_in = starts + jnp.exp(lead)[:, :, None, None] * acc_s[None]
    back = lax.all_to_all(chip_in.astype(bf16), "z", 0, 0, tiled=True)
    entry = back.astype(f32).reshape(half, state, width)

    into_second = jnp.exp(t_first)[:, None, None] * entry + first
    keep = jnp.where(c_idx == 0, entry, into_second).astype(bf16)
    send = jnp.where(c_idx == 0, into_second, entry).astype(bf16)
    other = swap(send)
    carried_in = jnp.where(
        c_idx == 0,
        jnp.concatenate([keep, other], axis=0),
        jnp.concatenate([other, keep], axis=0),
    )

    outside = jnp.einsum(
        "tgn,ghnp->tghp", c, carried_in.reshape(G, per_group, state, width),
        preferred_element_type=f32,
    ).reshape(tokens, heads, width)
    mixed = inside + jnp.exp(within)[..., None] * outside + skip[None, :, None] * x.astype(f32)
    return mixed.astype(bf16).reshape(tokens, heads * width)


def solution(mesh):
    n_seq, n_head = mesh.devices.shape
    grid = Mesh(mesh.devices.reshape(n_seq, n_head // CORES, CORES), ("seq", "z", "core"))
    rows = P(("seq", "z", "core"), None)
    in_specs = (rows, rows, rows, rows, rows, P(("z", "core")))
    return jax.shard_map(local, mesh=grid, in_specs=in_specs, out_specs=rows, check_vma=False)
```

```python
import jax
import jax.numpy as jnp
from jax import lax
from jax.sharding import Mesh
from jax.sharding import PartitionSpec as P

G = 8
CORES = 2


def swap(value):
    return lax.ppermute(value, "core", [(0, 1), (1, 0)])


def split3(value):
    hi = lax.reduce_precision(value, exponent_bits=8, mantissa_bits=7)
    rest = value - hi
    mid = lax.reduce_precision(rest, exponent_bits=8, mantissa_bits=7)
    return jnp.stack([hi, mid, rest - mid], axis=-1).astype(jnp.bfloat16)


def join3(parts):
    parts = parts.astype(jnp.float32)
    return (parts[..., 0] + parts[..., 1]) + parts[..., 2]


def lower_mask(outs, ins):
    return (jnp.arange(ins)[None, :] < jnp.arange(outs)[:, None]).astype(jnp.float32)


def decay_matrix(totals, outs):
    count = totals.shape[0]
    a = jnp.arange(outs)[:, None, None]
    b = jnp.arange(count)[None, :, None]
    m = jnp.arange(count)[None, None, :]
    between = ((b < m) & (m < a)).astype(jnp.float32)
    exponent = jnp.einsum("abm,mh->hab", between, totals, precision=lax.Precision.HIGHEST)
    earlier = (b < a)[None, :, :, 0]
    return jnp.where(earlier, jnp.exp(jnp.where(earlier, exponent, 0.0)), 0.0)


def local(features, increment_per_head, token_log_decay, b_matrix, c_matrix, skip_gain):
    f32, bf16 = jnp.float32, jnp.bfloat16
    n_seq = lax.axis_size("seq")
    n_z = lax.axis_size("z")
    n_core = lax.axis_size("core")
    z_idx = lax.axis_index("z")
    c_idx = lax.axis_index("core")
    tokens = features.shape[0]
    heads = increment_per_head.shape[1]
    width = features.shape[1] // heads
    state = b_matrix.shape[1] // G
    per_group = heads // G
    half = heads // n_core
    quarter = half // n_z

    x = features.reshape(tokens, heads, width)
    step = increment_per_head.astype(f32)
    within = jnp.cumsum(token_log_decay.astype(f32), axis=0)
    total = within[-1]
    b = b_matrix.reshape(tokens, G, state)
    c = c_matrix.reshape(tokens, G, state)
    partner = swap(jnp.concatenate([total, skip_gain.astype(f32)]))
    t_first = jnp.where(c_idx == 0, total, partner[:heads])
    t_second = jnp.where(c_idx == 0, partner[:heads], total)
    chip_skip = jnp.where(
        c_idx == 0,
        jnp.concatenate([skip_gain.astype(f32), partner[heads:]]),
        jnp.concatenate([partner[heads:], skip_gain.astype(f32)]),
    )

    factor = jnp.exp(total[None, :] - within) * step
    scaled = (x * factor[..., None]).astype(bf16)
    update = jnp.einsum(
        "sgn,sghp->ghnp", b, scaled.reshape(tokens, G, per_group, width),
        preferred_element_type=f32,
    ).reshape(heads, state, width)

    own = lax.dynamic_slice_in_dim(update, c_idx * half, half, 0)
    got = swap(lax.dynamic_slice_in_dim(update, (1 - c_idx) * half, half, 0))
    first = jnp.where(c_idx == 0, own, got)
    second = jnp.where(c_idx == 0, got, own)
    t_first = lax.dynamic_slice_in_dim(t_first, c_idx * half, half)
    t_second = lax.dynamic_slice_in_dim(t_second, c_idx * half, half)
    pair = jnp.exp(t_second)[:, None, None] * first + second

    pair = pair.astype(bf16).reshape(n_z, quarter, state, width)
    per_chip = chip_skip.shape[0]
    extra = jnp.concatenate(
        [
            split3((t_first + t_second).reshape(n_z, quarter)),
            jnp.broadcast_to(
                split3(chip_skip.reshape(quarter, per_chip // quarter)).reshape(1, quarter, -1),
                (n_z, quarter, 3 * per_chip // quarter),
            ),
        ],
        axis=-1,
    )
    extra = jnp.pad(
        extra, ((0, 0), (0, state - quarter), (0, width - extra.shape[-1]))
    )
    message = jnp.concatenate([pair, extra[:, None]], axis=1)
    rows = lax.all_to_all(message, "z", 0, 0, tiled=True)
    scores = jnp.einsum("tgn,sgn->gts", c, b, preferred_element_type=f32)
    scores = jnp.repeat(scores, per_group, axis=0)
    causal = (jnp.arange(tokens)[:, None] >= jnp.arange(tokens)[None, :])[None]
    w_t = within.T
    gap = w_t[:, :, None] - w_t[:, None, :]
    damping = jnp.where(causal, jnp.exp(jnp.where(causal, gap, 0.0)), 0.0)
    weight = (scores * damping * step.T[:, None, :]).astype(bf16)
    inside = jnp.einsum("hts,shp->thp", weight, x, preferred_element_type=f32)

    chip_totals = join3(rows[:, quarter, :quarter, 0:3])
    inside, chip_totals = lax.optimization_barrier((inside, chip_totals))
    skip = join3(
        rows[:, quarter, :quarter, 3 : 3 + 3 * per_chip // quarter].reshape(
            n_z, quarter, -1, 3
        )
    ).reshape(heads)
    scan = jnp.einsum(
        "hab,bhnp->ahnp",
        decay_matrix(chip_totals, n_z + 1),
        rows[:, :quarter].astype(f32),
        precision=lax.Precision.HIGHEST,
    )
    leads = jnp.einsum(
        "am,mh->ah", lower_mask(n_z + 1, n_z), chip_totals, precision=lax.Precision.HIGHEST
    )
    starts, run = scan[:n_z], scan[n_z]
    lead, before = leads[:n_z], leads[n_z]

    per = quarter * width // n_seq
    chunks = run.transpose(0, 2, 1).reshape(n_seq, per, state)
    row_totals = jnp.repeat(before, width).reshape(n_seq, per)
    packed = jnp.concatenate(
        [chunks, jnp.pad(row_totals, ((0, 0), (0, state - per)))[:, None, :]], axis=1
    )
    gathered = lax.all_to_all(packed, "seq", 0, 0, tiled=True)
    entering = jnp.einsum(
        "rab,brn->arn",
        decay_matrix(gathered[:, per, :per], n_seq),
        gathered[:, :per],
        precision=lax.Precision.HIGHEST,
    )
    acc_s = lax.all_to_all(entering, "seq", 0, 0, tiled=True)
    acc_s = acc_s.reshape(quarter, width, state).transpose(0, 2, 1)

    chip_in = starts + jnp.exp(lead)[:, :, None, None] * acc_s[None]
    back = lax.all_to_all(chip_in.astype(bf16), "z", 0, 0, tiled=True)
    entry = back.astype(f32).reshape(half, state, width)

    into_second = jnp.exp(t_first)[:, None, None] * entry + first
    keep = jnp.where(c_idx == 0, entry, into_second).astype(bf16)
    send = jnp.where(c_idx == 0, into_second, entry).astype(bf16)
    other = swap(send)

    groups = G // n_core
    c_keep = lax.dynamic_slice_in_dim(c, c_idx * groups, groups, 1)
    c_other = lax.dynamic_slice_in_dim(c, (1 - c_idx) * groups, groups, 1)
    out_keep = jnp.einsum(
        "tgn,ghnp->tghp", c_keep, keep.reshape(groups, per_group, state, width),
        preferred_element_type=f32,
    ).reshape(tokens, half * width)
    out_other = jnp.einsum(
        "tgn,ghnp->tghp", c_other, other.reshape(groups, per_group, state, width),
        preferred_element_type=f32,
    ).reshape(tokens, half * width)
    outside = jnp.where(
        c_idx == 0,
        jnp.concatenate([out_keep, out_other], axis=1),
        jnp.concatenate([out_other, out_keep], axis=1),
    )
    decay_in = jnp.repeat(jnp.exp(within), width, axis=1)
    gain = jnp.repeat(skip, width)[None, :]
    mixed = (
        inside.reshape(tokens, heads * width)
        + decay_in * outside
        + gain * features.astype(f32)
    )
    return mixed.astype(bf16)


def solution(mesh):
    n_seq, n_head = mesh.devices.shape
    grid = Mesh(mesh.devices.reshape(n_seq, n_head // CORES, CORES), ("seq", "z", "core"))
    rows = P(("seq", "z", "core"), None)
    in_specs = (rows, rows, rows, rows, rows, P(("z", "core")))
    return jax.shard_map(local, mesh=grid, in_specs=in_specs, out_specs=rows, check_vma=False)
```

```python
import jax
import jax.numpy as jnp
from jax import lax
from jax.sharding import Mesh
from jax.sharding import PartitionSpec as P

G = 8
CORES = 2


def swap(value):
    return lax.ppermute(value, "core", [(0, 1), (1, 0)])


def split3(value):
    hi = lax.reduce_precision(value, exponent_bits=8, mantissa_bits=7)
    rest = value - hi
    mid = lax.reduce_precision(rest, exponent_bits=8, mantissa_bits=7)
    return jnp.stack([hi, mid, rest - mid], axis=-1).astype(jnp.bfloat16)


def join3(parts):
    parts = parts.astype(jnp.float32)
    return (parts[..., 0] + parts[..., 1]) + parts[..., 2]


def lower_mask(outs, ins):
    return (jnp.arange(ins)[None, :] < jnp.arange(outs)[:, None]).astype(jnp.float32)


def decay_matrix(totals, outs):
    count = totals.shape[0]
    a = jnp.arange(outs)[:, None, None]
    b = jnp.arange(count)[None, :, None]
    m = jnp.arange(count)[None, None, :]
    between = ((b < m) & (m < a)).astype(jnp.float32)
    exponent = jnp.einsum("abm,mh->hab", between, totals, precision=lax.Precision.HIGHEST)
    earlier = (b < a)[None, :, :, 0]
    return jnp.where(earlier, jnp.exp(jnp.where(earlier, exponent, 0.0)), 0.0)


def local(features, increment_per_head, token_log_decay, b_matrix, c_matrix, skip_gain):
    f32, bf16 = jnp.float32, jnp.bfloat16
    n_seq = lax.axis_size("seq")
    n_z = lax.axis_size("z")
    n_core = lax.axis_size("core")
    z_idx = lax.axis_index("z")
    c_idx = lax.axis_index("core")
    tokens = features.shape[0]
    heads = increment_per_head.shape[1]
    width = features.shape[1] // heads
    state = b_matrix.shape[1] // G
    per_group = heads // G
    half = heads // n_core
    quarter = half // n_z

    x = features.reshape(tokens, heads, width)
    step = increment_per_head.astype(f32)
    within = jnp.cumsum(token_log_decay.astype(f32), axis=0)
    total = within[-1]
    b = b_matrix.reshape(tokens, G, state)
    c = c_matrix.reshape(tokens, G, state)
    factor = jnp.exp(total[None, :] - within) * step
    scaled = (x * factor[..., None]).astype(bf16)
    update = jnp.einsum(
        "sgn,sghp->ghnp", b, scaled.reshape(tokens, G, per_group, width),
        preferred_element_type=f32,
    ).reshape(heads, state, width)

    own = lax.dynamic_slice_in_dim(update, c_idx * half, half, 0)
    small = jnp.zeros((state, width), f32).at[:heads, 0].set(total)
    small = small.at[: skip_gain.shape[0], 1].set(skip_gain.astype(f32))
    got = swap(
        jnp.concatenate(
            [lax.dynamic_slice_in_dim(update, (1 - c_idx) * half, half, 0), small[None]], axis=0
        )
    )
    partner = jnp.concatenate([got[half, :heads, 0], got[half, : skip_gain.shape[0], 1]])
    got = got[:half]
    t_first = jnp.where(c_idx == 0, total, partner[:heads])
    t_second = jnp.where(c_idx == 0, partner[:heads], total)
    chip_skip = jnp.where(
        c_idx == 0,
        jnp.concatenate([skip_gain.astype(f32), partner[heads:]]),
        jnp.concatenate([partner[heads:], skip_gain.astype(f32)]),
    )

    first = jnp.where(c_idx == 0, own, got)
    second = jnp.where(c_idx == 0, got, own)
    t_first = lax.dynamic_slice_in_dim(t_first, c_idx * half, half)
    t_second = lax.dynamic_slice_in_dim(t_second, c_idx * half, half)
    pair = jnp.exp(t_second)[:, None, None] * first + second

    pair = pair.astype(bf16).reshape(n_z, quarter, state, width)
    per_chip = chip_skip.shape[0]
    extra = jnp.concatenate(
        [
            split3((t_first + t_second).reshape(n_z, quarter)),
            jnp.broadcast_to(
                split3(chip_skip.reshape(quarter, per_chip // quarter)).reshape(1, quarter, -1),
                (n_z, quarter, 3 * per_chip // quarter),
            ),
        ],
        axis=-1,
    )
    extra = jnp.pad(
        extra, ((0, 0), (0, state - quarter), (0, width - extra.shape[-1]))
    )
    message = jnp.concatenate([pair, extra[:, None]], axis=1)
    rows = lax.all_to_all(message, "z", 0, 0, tiled=True)
    scores = jnp.einsum("tgn,sgn->gts", c, b, preferred_element_type=f32)
    scores = jnp.repeat(scores, per_group, axis=0)
    causal = (jnp.arange(tokens)[:, None] >= jnp.arange(tokens)[None, :])[None]
    w_t = within.T
    gap = w_t[:, :, None] - w_t[:, None, :]
    damping = jnp.where(causal, jnp.exp(jnp.where(causal, gap, 0.0)), 0.0)
    weight = (scores * damping * step.T[:, None, :]).astype(bf16)
    inside = jnp.einsum("hts,shp->thp", weight, x, preferred_element_type=f32)

    chip_totals = join3(rows[:, quarter, :quarter, 0:3])
    inside, chip_totals = lax.optimization_barrier((inside, chip_totals))
    skip = join3(
        rows[:, quarter, :quarter, 3 : 3 + 3 * per_chip // quarter].reshape(
            n_z, quarter, -1, 3
        )
    ).reshape(heads)
    scan = jnp.einsum(
        "hab,bhnp->ahnp",
        decay_matrix(chip_totals, n_z + 1),
        rows[:, :quarter].astype(f32),
        precision=lax.Precision.HIGHEST,
    )
    leads = jnp.einsum(
        "am,mh->ah", lower_mask(n_z + 1, n_z), chip_totals, precision=lax.Precision.HIGHEST
    )
    starts, run = scan[:n_z], scan[n_z]
    lead, before = leads[:n_z], leads[n_z]

    per = quarter * width // n_seq
    chunks = run.transpose(0, 2, 1).reshape(n_seq, per, state)
    row_totals = jnp.repeat(before, width).reshape(n_seq, per)
    packed = jnp.concatenate(
        [chunks, jnp.pad(row_totals, ((0, 0), (0, state - per)))[:, None, :]], axis=1
    )
    gathered = lax.all_to_all(packed, "seq", 0, 0, tiled=True)
    entering = jnp.einsum(
        "rab,brn->arn",
        decay_matrix(gathered[:, per, :per], n_seq),
        gathered[:, :per],
        precision=lax.Precision.HIGHEST,
    )
    acc_s = lax.all_to_all(entering, "seq", 0, 0, tiled=True)
    acc_s = acc_s.reshape(quarter, width, state).transpose(0, 2, 1)

    chip_in = starts + jnp.exp(lead)[:, :, None, None] * acc_s[None]
    back = lax.all_to_all(chip_in.astype(bf16), "z", 0, 0, tiled=True)
    entry = back.astype(f32).reshape(half, state, width)

    into_second = jnp.exp(t_first)[:, None, None] * entry + first
    keep = jnp.where(c_idx == 0, entry, into_second).astype(bf16)
    send = jnp.where(c_idx == 0, into_second, entry).astype(bf16)
    other = swap(send)
    carried_in = jnp.where(
        c_idx == 0,
        jnp.concatenate([keep, other], axis=0),
        jnp.concatenate([other, keep], axis=0),
    )

    outside = jnp.einsum(
        "tgn,ghnp->tghp", c, carried_in.reshape(G, per_group, state, width),
        preferred_element_type=f32,
    ).reshape(tokens, heads, width)
    mixed = inside + jnp.exp(within)[..., None] * outside + skip[None, :, None] * x.astype(f32)
    return mixed.astype(bf16).reshape(tokens, heads * width)


def solution(mesh):
    n_seq, n_head = mesh.devices.shape
    grid = Mesh(mesh.devices.reshape(n_seq, n_head // CORES, CORES), ("seq", "z", "core"))
    rows = P(("seq", "z", "core"), None)
    in_specs = (rows, rows, rows, rows, rows, P(("z", "core")))
    return jax.shard_map(local, mesh=grid, in_specs=in_specs, out_specs=rows, check_vma=False)
```

```python
import jax
import jax.numpy as jnp
from jax import lax
from jax.sharding import Mesh
from jax.sharding import PartitionSpec as P

G = 8
CORES = 2


def swap(value):
    return lax.ppermute(value, "core", [(0, 1), (1, 0)])


def split3(value):
    hi = lax.reduce_precision(value, exponent_bits=8, mantissa_bits=7)
    rest = value - hi
    mid = lax.reduce_precision(rest, exponent_bits=8, mantissa_bits=7)
    return jnp.stack([hi, mid, rest - mid], axis=-1).astype(jnp.bfloat16)


def join3(parts):
    parts = parts.astype(jnp.float32)
    return (parts[..., 0] + parts[..., 1]) + parts[..., 2]


def lower_mask(outs, ins):
    return (jnp.arange(ins)[None, :] < jnp.arange(outs)[:, None]).astype(jnp.float32)


def decay_matrix(totals, outs):
    count = totals.shape[0]
    a = jnp.arange(outs)[:, None, None]
    b = jnp.arange(count)[None, :, None]
    m = jnp.arange(count)[None, None, :]
    between = ((b < m) & (m < a)).astype(jnp.float32)
    exponent = jnp.einsum("abm,mh->hab", between, totals, precision=lax.Precision.HIGHEST)
    earlier = (b < a)[None, :, :, 0]
    return jnp.where(earlier, jnp.exp(jnp.where(earlier, exponent, 0.0)), 0.0)


def local(features, increment_per_head, token_log_decay, b_matrix, c_matrix, skip_gain):
    f32, bf16 = jnp.float32, jnp.bfloat16
    n_seq = lax.axis_size("seq")
    n_z = lax.axis_size("z")
    n_core = lax.axis_size("core")
    z_idx = lax.axis_index("z")
    c_idx = lax.axis_index("core")
    tokens = features.shape[0]
    heads = increment_per_head.shape[1]
    width = features.shape[1] // heads
    state = b_matrix.shape[1] // G
    per_group = heads // G
    half = heads // n_core
    quarter = half // n_z

    x = features.reshape(tokens, heads, width)
    step = increment_per_head.astype(f32)
    within = jnp.cumsum(token_log_decay.astype(f32), axis=0)
    total = within[-1]
    b = b_matrix.reshape(tokens, G, state)
    c = c_matrix.reshape(tokens, G, state)
    partner = swap(jnp.concatenate([total, skip_gain.astype(f32)]))
    t_first = jnp.where(c_idx == 0, total, partner[:heads])
    t_second = jnp.where(c_idx == 0, partner[:heads], total)
    chip_skip = jnp.where(
        c_idx == 0,
        jnp.concatenate([skip_gain.astype(f32), partner[heads:]]),
        jnp.concatenate([partner[heads:], skip_gain.astype(f32)]),
    )

    factor = jnp.exp(total[None, :] - within) * step
    scaled = (x * factor[..., None]).astype(bf16)
    update = jnp.einsum(
        "sgn,sghp->ghnp", b, scaled.reshape(tokens, G, per_group, width),
        preferred_element_type=f32,
    ).reshape(heads, state, width)

    own = lax.dynamic_slice_in_dim(update, c_idx * half, half, 0)
    got = swap(
        lax.dynamic_slice_in_dim(update, (1 - c_idx) * half, half, 0).astype(bf16)
    ).astype(f32)
    first = jnp.where(c_idx == 0, own, got)
    second = jnp.where(c_idx == 0, got, own)
    t_first = lax.dynamic_slice_in_dim(t_first, c_idx * half, half)
    t_second = lax.dynamic_slice_in_dim(t_second, c_idx * half, half)
    pair = jnp.exp(t_second)[:, None, None] * first + second

    pair = pair.astype(bf16).reshape(n_z, quarter, state, width)
    per_chip = chip_skip.shape[0]
    extra = jnp.concatenate(
        [
            split3((t_first + t_second).reshape(n_z, quarter)),
            jnp.broadcast_to(
                split3(chip_skip.reshape(quarter, per_chip // quarter)).reshape(1, quarter, -1),
                (n_z, quarter, 3 * per_chip // quarter),
            ),
        ],
        axis=-1,
    )
    extra = jnp.pad(
        extra, ((0, 0), (0, state - quarter), (0, width - extra.shape[-1]))
    )
    message = jnp.concatenate([pair, extra[:, None]], axis=1)
    rows = lax.all_to_all(message, "z", 0, 0, tiled=True)
    scores = jnp.einsum("tgn,sgn->gts", c, b, preferred_element_type=f32)
    scores = jnp.repeat(scores, per_group, axis=0)
    causal = (jnp.arange(tokens)[:, None] >= jnp.arange(tokens)[None, :])[None]
    w_t = within.T
    gap = w_t[:, :, None] - w_t[:, None, :]
    damping = jnp.where(causal, jnp.exp(jnp.where(causal, gap, 0.0)), 0.0)
    weight = (scores * damping * step.T[:, None, :]).astype(bf16)
    inside = jnp.einsum("hts,shp->thp", weight, x, preferred_element_type=f32)

    chip_totals = join3(rows[:, quarter, :quarter, 0:3])
    inside, chip_totals = lax.optimization_barrier((inside, chip_totals))
    skip = join3(
        rows[:, quarter, :quarter, 3 : 3 + 3 * per_chip // quarter].reshape(
            n_z, quarter, -1, 3
        )
    ).reshape(heads)
    scan = jnp.einsum(
        "hab,bhnp->ahnp",
        decay_matrix(chip_totals, n_z + 1),
        rows[:, :quarter].astype(f32),
        precision=lax.Precision.HIGH,
    )
    leads = jnp.einsum(
        "am,mh->ah", lower_mask(n_z + 1, n_z), chip_totals, precision=lax.Precision.HIGHEST
    )
    starts, run = scan[:n_z], scan[n_z]
    lead, before = leads[:n_z], leads[n_z]

    per = quarter * width // n_seq
    chunks = run.transpose(0, 2, 1).reshape(n_seq, per, state)
    row_totals = jnp.repeat(before, width).reshape(n_seq, per)
    packed = jnp.concatenate(
        [chunks, jnp.pad(row_totals, ((0, 0), (0, state - per)))[:, None, :]], axis=1
    )
    gathered = lax.all_to_all(packed, "seq", 0, 0, tiled=True)
    entering = jnp.einsum(
        "rab,brn->arn",
        decay_matrix(gathered[:, per, :per], n_seq),
        gathered[:, :per],
        precision=lax.Precision.HIGH,
    )
    acc_s = lax.all_to_all(entering, "seq", 0, 0, tiled=True)
    acc_s = acc_s.reshape(quarter, width, state).transpose(0, 2, 1)

    chip_in = starts + jnp.exp(lead)[:, :, None, None] * acc_s[None]
    back = lax.all_to_all(chip_in.astype(bf16), "z", 0, 0, tiled=True)
    entry = back.astype(f32).reshape(half, state, width)

    into_second = jnp.exp(t_first)[:, None, None] * entry + first
    keep = jnp.where(c_idx == 0, entry, into_second).astype(bf16)
    send = jnp.where(c_idx == 0, into_second, entry).astype(bf16)
    other = swap(send)
    carried_in = jnp.where(
        c_idx == 0,
        jnp.concatenate([keep, other], axis=0),
        jnp.concatenate([other, keep], axis=0),
    )

    outside = jnp.einsum(
        "tgn,ghnp->tghp", c, carried_in.reshape(G, per_group, state, width),
        preferred_element_type=f32,
    ).reshape(tokens, heads, width)
    mixed = inside + jnp.exp(within)[..., None] * outside + skip[None, :, None] * x.astype(f32)
    return mixed.astype(bf16).reshape(tokens, heads * width)


def solution(mesh):
    n_seq, n_head = mesh.devices.shape
    grid = Mesh(mesh.devices.reshape(n_seq, n_head // CORES, CORES), ("seq", "z", "core"))
    rows = P(("seq", "z", "core"), None)
    in_specs = (rows, rows, rows, rows, rows, P(("z", "core")))
    return jax.shard_map(local, mesh=grid, in_specs=in_specs, out_specs=rows, check_vma=False)
```

```python
import jax
import jax.numpy as jnp
from jax import lax
from jax.sharding import Mesh
from jax.sharding import PartitionSpec as P

G = 8
CORES = 2


def swap(value):
    return lax.ppermute(value, "core", [(0, 1), (1, 0)])


def split3(value):
    hi = lax.reduce_precision(value, exponent_bits=8, mantissa_bits=7)
    rest = value - hi
    mid = lax.reduce_precision(rest, exponent_bits=8, mantissa_bits=7)
    return jnp.stack([hi, mid, rest - mid], axis=-1).astype(jnp.bfloat16)


def join3(parts):
    parts = parts.astype(jnp.float32)
    return (parts[..., 0] + parts[..., 1]) + parts[..., 2]


def lower_mask(outs, ins):
    return (jnp.arange(ins)[None, :] < jnp.arange(outs)[:, None]).astype(jnp.float32)


def decay_matrix(totals, outs):
    count = totals.shape[0]
    a = jnp.arange(outs)[:, None, None]
    b = jnp.arange(count)[None, :, None]
    m = jnp.arange(count)[None, None, :]
    between = ((b < m) & (m < a)).astype(jnp.float32)
    exponent = jnp.einsum("abm,mh->hab", between, totals, precision=lax.Precision.HIGHEST)
    earlier = (b < a)[None, :, :, 0]
    return jnp.where(earlier, jnp.exp(jnp.where(earlier, exponent, 0.0)), 0.0)


def local(features, increment_per_head, token_log_decay, b_matrix, c_matrix, skip_gain):
    f32, bf16 = jnp.float32, jnp.bfloat16
    n_seq = lax.axis_size("seq")
    n_z = lax.axis_size("z")
    n_core = lax.axis_size("core")
    z_idx = lax.axis_index("z")
    c_idx = lax.axis_index("core")
    tokens = features.shape[0]
    heads = increment_per_head.shape[1]
    width = features.shape[1] // heads
    state = b_matrix.shape[1] // G
    per_group = heads // G
    half = heads // n_core
    quarter = half // n_z

    x = features.reshape(tokens, heads, width)
    step = increment_per_head.astype(f32)
    within = jnp.cumsum(token_log_decay.astype(f32), axis=0)
    total = within[-1]
    b = b_matrix.reshape(tokens, G, state)
    c = c_matrix.reshape(tokens, G, state)
    partner = swap(jnp.concatenate([total, skip_gain.astype(f32)]))
    t_first = jnp.where(c_idx == 0, total, partner[:heads])
    t_second = jnp.where(c_idx == 0, partner[:heads], total)
    chip_skip = jnp.where(
        c_idx == 0,
        jnp.concatenate([skip_gain.astype(f32), partner[heads:]]),
        jnp.concatenate([partner[heads:], skip_gain.astype(f32)]),
    )

    factor = jnp.exp(total[None, :] - within) * step
    scaled = (x * factor[..., None]).astype(bf16)
    update = jnp.einsum(
        "sgn,sghp->ghnp", b, scaled.reshape(tokens, G, per_group, width),
        preferred_element_type=f32,
    ).reshape(heads, state, width)

    own = lax.dynamic_slice_in_dim(update, c_idx * half, half, 0)
    got = swap(lax.dynamic_slice_in_dim(update, (1 - c_idx) * half, half, 0))
    first = jnp.where(c_idx == 0, own, got)
    second = jnp.where(c_idx == 0, got, own)
    t_first = lax.dynamic_slice_in_dim(t_first, c_idx * half, half)
    t_second = lax.dynamic_slice_in_dim(t_second, c_idx * half, half)
    pair = jnp.exp(t_second)[:, None, None] * first + second

    pair = pair.astype(bf16).reshape(n_z, quarter, state, width)
    per_chip = chip_skip.shape[0]
    extra = jnp.concatenate(
        [
            split3((t_first + t_second).reshape(n_z, quarter)),
            jnp.broadcast_to(
                split3(chip_skip.reshape(quarter, per_chip // quarter)).reshape(1, quarter, -1),
                (n_z, quarter, 3 * per_chip // quarter),
            ),
        ],
        axis=-1,
    )
    extra = jnp.pad(
        extra, ((0, 0), (0, state - quarter), (0, width - extra.shape[-1]))
    )
    message = jnp.concatenate([pair, extra[:, None]], axis=1)
    rows = lax.all_to_all(message, "z", 0, 0, tiled=True)
    scores = jnp.einsum("tgn,sgn->gts", c, b, preferred_element_type=f32)
    scores = jnp.repeat(scores, per_group, axis=0)
    causal = (jnp.arange(tokens)[:, None] >= jnp.arange(tokens)[None, :])[None]
    w_t = within.T
    gap = w_t[:, :, None] - w_t[:, None, :]
    damping = jnp.where(causal, jnp.exp(jnp.where(causal, gap, 0.0)), 0.0)
    weight = (scores * damping * step.T[:, None, :]).astype(bf16)
    inside = jnp.einsum("hts,shp->thp", weight, x, preferred_element_type=f32)

    chip_totals = join3(rows[:, quarter, :quarter, 0:3])
    inside, chip_totals = lax.optimization_barrier((inside, chip_totals))
    skip = join3(
        rows[:, quarter, :quarter, 3 : 3 + 3 * per_chip // quarter].reshape(
            n_z, quarter, -1, 3
        )
    ).reshape(heads)
    scan = jnp.einsum(
        "hab,bhnp->ahnp",
        decay_matrix(chip_totals, n_z + 1),
        rows[:, :quarter].astype(f32),
        precision=lax.Precision.HIGHEST,
    )
    leads = jnp.einsum(
        "am,mh->ah", lower_mask(n_z + 1, n_z), chip_totals, precision=lax.Precision.HIGHEST
    )
    starts, run = scan[:n_z], scan[n_z]
    lead, before = leads[:n_z], leads[n_z]

    per = quarter * width // n_seq
    chunks = run.transpose(0, 2, 1).reshape(n_seq, per, state)
    row_totals = jnp.repeat(before, width).reshape(n_seq, per)
    packed = jnp.concatenate(
        [chunks, jnp.pad(row_totals, ((0, 0), (0, state - per)))[:, None, :]], axis=1
    )
    packed = jnp.pad(packed, ((0, 0), (0, -(per + 1) % 8), (0, 0)))
    gathered = lax.all_to_all(packed, "seq", 0, 0, tiled=True)
    entering = jnp.einsum(
        "rab,brn->arn",
        decay_matrix(gathered[:, per, :per], n_seq),
        gathered[:, :per],
        precision=lax.Precision.HIGHEST,
    )
    acc_s = lax.all_to_all(entering, "seq", 0, 0, tiled=True)
    acc_s = acc_s.reshape(quarter, width, state).transpose(0, 2, 1)

    chip_in = starts + jnp.exp(lead)[:, :, None, None] * acc_s[None]
    back = lax.all_to_all(chip_in.astype(bf16), "z", 0, 0, tiled=True)
    entry = back.astype(f32).reshape(half, state, width)

    into_second = jnp.exp(t_first)[:, None, None] * entry + first
    keep = jnp.where(c_idx == 0, entry, into_second).astype(bf16)
    send = jnp.where(c_idx == 0, into_second, entry).astype(bf16)
    other = swap(send)
    carried_in = jnp.where(
        c_idx == 0,
        jnp.concatenate([keep, other], axis=0),
        jnp.concatenate([other, keep], axis=0),
    )

    outside = jnp.einsum(
        "tgn,ghnp->tghp", c, carried_in.reshape(G, per_group, state, width),
        preferred_element_type=f32,
    ).reshape(tokens, heads, width)
    mixed = inside + jnp.exp(within)[..., None] * outside + skip[None, :, None] * x.astype(f32)
    return mixed.astype(bf16).reshape(tokens, heads * width)


def solution(mesh):
    n_seq, n_head = mesh.devices.shape
    grid = Mesh(mesh.devices.reshape(n_seq, n_head // CORES, CORES), ("seq", "z", "core"))
    rows = P(("seq", "z", "core"), None)
    in_specs = (rows, rows, rows, rows, rows, P(("z", "core")))
    return jax.shard_map(local, mesh=grid, in_specs=in_specs, out_specs=rows, check_vma=False)
```

```python
import jax
import jax.numpy as jnp
from jax import lax
from jax.sharding import Mesh
from jax.sharding import PartitionSpec as P

G = 8
CORES = 2


def swap(value):
    return lax.ppermute(value, "core", [(0, 1), (1, 0)])


def split3(value):
    hi = lax.reduce_precision(value, exponent_bits=8, mantissa_bits=7)
    rest = value - hi
    mid = lax.reduce_precision(rest, exponent_bits=8, mantissa_bits=7)
    return jnp.stack([hi, mid, rest - mid], axis=-1).astype(jnp.bfloat16)


def join3(parts):
    parts = parts.astype(jnp.float32)
    return (parts[..., 0] + parts[..., 1]) + parts[..., 2]


def lower_mask(outs, ins):
    return (jnp.arange(ins)[None, :] < jnp.arange(outs)[:, None]).astype(jnp.float32)


def decay_matrix(totals, outs):
    count = totals.shape[0]
    a = jnp.arange(outs)[:, None, None]
    b = jnp.arange(count)[None, :, None]
    m = jnp.arange(count)[None, None, :]
    between = ((b < m) & (m < a)).astype(jnp.float32)
    exponent = jnp.einsum("abm,mh->hab", between, totals, precision=lax.Precision.HIGHEST)
    earlier = (b < a)[None, :, :, 0]
    return jnp.where(earlier, jnp.exp(jnp.where(earlier, exponent, 0.0)), 0.0)


def local(features, increment_per_head, token_log_decay, b_matrix, c_matrix, skip_gain):
    f32, bf16 = jnp.float32, jnp.bfloat16
    n_seq = lax.axis_size("seq")
    n_z = lax.axis_size("z")
    n_core = lax.axis_size("core")
    z_idx = lax.axis_index("z")
    c_idx = lax.axis_index("core")
    tokens = features.shape[0]
    heads = increment_per_head.shape[1]
    width = features.shape[1] // heads
    state = b_matrix.shape[1] // G
    per_group = heads // G
    half = heads // n_core
    quarter = half // n_z

    x = features.reshape(tokens, heads, width)
    step = increment_per_head.astype(f32)
    within = jnp.cumsum(token_log_decay.astype(f32), axis=0)
    total = within[-1]
    b = b_matrix.reshape(tokens, G, state)
    c = c_matrix.reshape(tokens, G, state)
    partner = swap(jnp.concatenate([total, skip_gain.astype(f32)]))
    t_first = jnp.where(c_idx == 0, total, partner[:heads])
    t_second = jnp.where(c_idx == 0, partner[:heads], total)
    chip_skip = jnp.where(
        c_idx == 0,
        jnp.concatenate([skip_gain.astype(f32), partner[heads:]]),
        jnp.concatenate([partner[heads:], skip_gain.astype(f32)]),
    )

    factor = jnp.exp(total[None, :] - within) * step
    scaled = (x * factor[..., None]).astype(bf16)
    scaled = scaled.reshape(tokens, G, per_group, width)
    groups = G // n_core

    def update_of(core):
        return jnp.einsum(
            "sgn,sghp->ghnp",
            lax.dynamic_slice_in_dim(b, core * groups, groups, 1),
            lax.dynamic_slice_in_dim(scaled, core * groups, groups, 1),
            preferred_element_type=f32,
        ).reshape(half, state, width)

    own = update_of(c_idx)
    got = swap(update_of(1 - c_idx))
    first = jnp.where(c_idx == 0, own, got)
    second = jnp.where(c_idx == 0, got, own)
    t_first = lax.dynamic_slice_in_dim(t_first, c_idx * half, half)
    t_second = lax.dynamic_slice_in_dim(t_second, c_idx * half, half)
    pair = jnp.exp(t_second)[:, None, None] * first + second

    pair = pair.astype(bf16).reshape(n_z, quarter, state, width)
    per_chip = chip_skip.shape[0]
    extra = jnp.concatenate(
        [
            split3((t_first + t_second).reshape(n_z, quarter)),
            jnp.broadcast_to(
                split3(chip_skip.reshape(quarter, per_chip // quarter)).reshape(1, quarter, -1),
                (n_z, quarter, 3 * per_chip // quarter),
            ),
        ],
        axis=-1,
    )
    extra = jnp.pad(
        extra, ((0, 0), (0, state - quarter), (0, width - extra.shape[-1]))
    )
    message = jnp.concatenate([pair, extra[:, None]], axis=1)
    rows = lax.all_to_all(message, "z", 0, 0, tiled=True)
    scores = jnp.einsum("tgn,sgn->gts", c, b, preferred_element_type=f32)
    scores = jnp.repeat(scores, per_group, axis=0)
    causal = (jnp.arange(tokens)[:, None] >= jnp.arange(tokens)[None, :])[None]
    w_t = within.T
    gap = w_t[:, :, None] - w_t[:, None, :]
    damping = jnp.where(causal, jnp.exp(jnp.where(causal, gap, 0.0)), 0.0)
    weight = (scores * damping * step.T[:, None, :]).astype(bf16)
    inside = jnp.einsum("hts,shp->thp", weight, x, preferred_element_type=f32)

    chip_totals = join3(rows[:, quarter, :quarter, 0:3])
    inside, chip_totals = lax.optimization_barrier((inside, chip_totals))
    skip = join3(
        rows[:, quarter, :quarter, 3 : 3 + 3 * per_chip // quarter].reshape(
            n_z, quarter, -1, 3
        )
    ).reshape(heads)
    scan = jnp.einsum(
        "hab,bhnp->ahnp",
        decay_matrix(chip_totals, n_z + 1),
        rows[:, :quarter].astype(f32),
        precision=lax.Precision.HIGHEST,
    )
    leads = jnp.einsum(
        "am,mh->ah", lower_mask(n_z + 1, n_z), chip_totals, precision=lax.Precision.HIGHEST
    )
    starts, run = scan[:n_z], scan[n_z]
    lead, before = leads[:n_z], leads[n_z]

    per = quarter * width // n_seq
    chunks = run.transpose(0, 2, 1).reshape(n_seq, per, state)
    row_totals = jnp.repeat(before, width).reshape(n_seq, per)
    packed = jnp.concatenate(
        [chunks, jnp.pad(row_totals, ((0, 0), (0, state - per)))[:, None, :]], axis=1
    )
    packed = jnp.pad(packed, ((0, 0), (0, -(per + 1) % 8), (0, 0)))
    gathered = lax.all_to_all(packed, "seq", 0, 0, tiled=True)
    entering = jnp.einsum(
        "rab,brn->arn",
        decay_matrix(gathered[:, per, :per], n_seq),
        gathered[:, :per],
        precision=lax.Precision.HIGHEST,
    )
    acc_s = lax.all_to_all(entering, "seq", 0, 0, tiled=True)
    acc_s = acc_s.reshape(quarter, width, state).transpose(0, 2, 1)

    chip_in = starts + jnp.exp(lead)[:, :, None, None] * acc_s[None]
    back = lax.all_to_all(chip_in.astype(bf16), "z", 0, 0, tiled=True)
    entry = back.astype(f32).reshape(half, state, width)

    into_second = jnp.exp(t_first)[:, None, None] * entry + first
    keep = jnp.where(c_idx == 0, entry, into_second).astype(bf16)
    send = jnp.where(c_idx == 0, into_second, entry).astype(bf16)
    other = swap(send)
    carried_in = jnp.where(
        c_idx == 0,
        jnp.concatenate([keep, other], axis=0),
        jnp.concatenate([other, keep], axis=0),
    )

    outside = jnp.einsum(
        "tgn,ghnp->tghp", c, carried_in.reshape(G, per_group, state, width),
        preferred_element_type=f32,
    ).reshape(tokens, heads, width)
    mixed = inside + jnp.exp(within)[..., None] * outside + skip[None, :, None] * x.astype(f32)
    return mixed.astype(bf16).reshape(tokens, heads * width)


def solution(mesh):
    n_seq, n_head = mesh.devices.shape
    grid = Mesh(mesh.devices.reshape(n_seq, n_head // CORES, CORES), ("seq", "z", "core"))
    rows = P(("seq", "z", "core"), None)
    in_specs = (rows, rows, rows, rows, rows, P(("z", "core")))
    return jax.shard_map(local, mesh=grid, in_specs=in_specs, out_specs=rows, check_vma=False)
```

```python
import jax
import jax.numpy as jnp
from jax import lax
from jax.sharding import Mesh
from jax.sharding import PartitionSpec as P

G = 8
CORES = 2


def swap(value):
    return lax.ppermute(value, "core", [(0, 1), (1, 0)])


def split3(value):
    hi = lax.reduce_precision(value, exponent_bits=8, mantissa_bits=7)
    rest = value - hi
    mid = lax.reduce_precision(rest, exponent_bits=8, mantissa_bits=7)
    return jnp.stack([hi, mid, rest - mid], axis=-1).astype(jnp.bfloat16)


def join3(parts):
    parts = parts.astype(jnp.float32)
    return (parts[..., 0] + parts[..., 1]) + parts[..., 2]


def lower_mask(outs, ins):
    return (jnp.arange(ins)[None, :] < jnp.arange(outs)[:, None]).astype(jnp.float32)


def decay_matrix(totals, outs):
    count = totals.shape[0]
    a = jnp.arange(outs)[:, None, None]
    b = jnp.arange(count)[None, :, None]
    m = jnp.arange(count)[None, None, :]
    between = ((b < m) & (m < a)).astype(jnp.float32)
    exponent = jnp.einsum("abm,mh->hab", between, totals, precision=lax.Precision.HIGHEST)
    earlier = (b < a)[None, :, :, 0]
    return jnp.where(earlier, jnp.exp(jnp.where(earlier, exponent, 0.0)), 0.0)


def local(features, increment_per_head, token_log_decay, b_matrix, c_matrix, skip_gain):
    f32, bf16 = jnp.float32, jnp.bfloat16
    n_seq = lax.axis_size("seq")
    n_z = lax.axis_size("z")
    n_core = lax.axis_size("core")
    z_idx = lax.axis_index("z")
    c_idx = lax.axis_index("core")
    tokens = features.shape[0]
    heads = increment_per_head.shape[1]
    width = features.shape[1] // heads
    state = b_matrix.shape[1] // G
    per_group = heads // G
    half = heads // n_core
    quarter = half // n_z

    x = features.reshape(tokens, heads, width)
    step = increment_per_head.astype(f32)
    within = jnp.cumsum(token_log_decay.astype(f32), axis=0)
    total = within[-1]
    b = b_matrix.reshape(tokens, G, state)
    c = c_matrix.reshape(tokens, G, state)
    partner = swap(jnp.concatenate([total, skip_gain.astype(f32)]))
    t_first = jnp.where(c_idx == 0, total, partner[:heads])
    t_second = jnp.where(c_idx == 0, partner[:heads], total)
    chip_skip = jnp.where(
        c_idx == 0,
        jnp.concatenate([skip_gain.astype(f32), partner[heads:]]),
        jnp.concatenate([partner[heads:], skip_gain.astype(f32)]),
    )

    factor = jnp.exp(total[None, :] - within) * step
    scaled = (x * factor[..., None]).astype(bf16)
    update = jnp.einsum(
        "sgn,sghp->ghnp", b, scaled.reshape(tokens, G, per_group, width),
        preferred_element_type=f32,
    ).reshape(heads, state, width)

    own = lax.dynamic_slice_in_dim(update, c_idx * half, half, 0)
    got = swap(lax.dynamic_slice_in_dim(update, (1 - c_idx) * half, half, 0))
    first = jnp.where(c_idx == 0, own, got)
    second = jnp.where(c_idx == 0, got, own)
    t_first = lax.dynamic_slice_in_dim(t_first, c_idx * half, half)
    t_second = lax.dynamic_slice_in_dim(t_second, c_idx * half, half)
    pair = jnp.exp(t_second)[:, None, None] * first + second

    pair = pair.astype(bf16).reshape(n_z, quarter, state, width)
    per_chip = chip_skip.shape[0]
    extra = jnp.concatenate(
        [
            split3((t_first + t_second).reshape(n_z, quarter)),
            jnp.broadcast_to(
                split3(chip_skip.reshape(quarter, per_chip // quarter)).reshape(1, quarter, -1),
                (n_z, quarter, 3 * per_chip // quarter),
            ),
        ],
        axis=-1,
    )
    extra = jnp.pad(
        extra, ((0, 0), (0, state - quarter), (0, width - extra.shape[-1]))
    )
    message = jnp.concatenate([pair, extra[:, None]], axis=1)
    rows = lax.all_to_all(message, "z", 0, 0, tiled=True)
    scores = jnp.einsum("tgn,sgn->gts", c, b, preferred_element_type=f32)
    scores = jnp.repeat(scores, per_group, axis=0)
    causal = (jnp.arange(tokens)[:, None] >= jnp.arange(tokens)[None, :])[None]
    w_t = within.T
    gap = w_t[:, :, None] - w_t[:, None, :]
    damping = jnp.where(causal, jnp.exp(jnp.where(causal, gap, 0.0)), 0.0)
    weight = (scores * damping * step.T[:, None, :]).astype(bf16)
    inside = jnp.einsum("hts,shp->thp", weight, x, preferred_element_type=f32)

    chip_totals = join3(rows[:, quarter, :quarter, 0:3])
    inside, chip_totals = lax.optimization_barrier((inside, chip_totals))
    skip = join3(
        rows[:, quarter, :quarter, 3 : 3 + 3 * per_chip // quarter].reshape(
            n_z, quarter, -1, 3
        )
    ).reshape(heads)
    scan = jnp.einsum(
        "hab,bhnp->ahnp",
        decay_matrix(chip_totals, n_z + 1),
        rows[:, :quarter].astype(f32),
        precision=lax.Precision.HIGHEST,
    )
    leads = jnp.einsum(
        "am,mh->ah", lower_mask(n_z + 1, n_z), chip_totals, precision=lax.Precision.HIGHEST
    )
    starts, run = scan[:n_z], scan[n_z]
    lead, before = leads[:n_z], leads[n_z]

    per = quarter * width // n_seq
    chunks = run.transpose(0, 2, 1).reshape(n_seq, per, state)
    row_totals = jnp.repeat(before, width).reshape(n_seq, per)
    packed = jnp.concatenate(
        [chunks, jnp.pad(row_totals, ((0, 0), (0, state - per)))[:, None, :]], axis=1
    )
    packed = jnp.pad(packed, ((0, 0), (0, -(per + 1) % 8), (0, 0)))
    gathered = lax.all_to_all(packed, "seq", 0, 0, tiled=True)
    entering = jnp.einsum(
        "rab,brn->arn",
        decay_matrix(gathered[:, per, :per], n_seq),
        gathered[:, :per],
        precision=lax.Precision.HIGHEST,
    )
    acc_s = lax.all_to_all(entering.astype(bf16), "seq", 0, 0, tiled=True).astype(f32)
    acc_s = acc_s.reshape(quarter, width, state).transpose(0, 2, 1)

    chip_in = starts + jnp.exp(lead)[:, :, None, None] * acc_s[None]
    back = lax.all_to_all(chip_in.astype(bf16), "z", 0, 0, tiled=True)
    entry = back.astype(f32).reshape(half, state, width)

    into_second = jnp.exp(t_first)[:, None, None] * entry + first
    keep = jnp.where(c_idx == 0, entry, into_second).astype(bf16)
    send = jnp.where(c_idx == 0, into_second, entry).astype(bf16)
    other = swap(send)
    carried_in = jnp.where(
        c_idx == 0,
        jnp.concatenate([keep, other], axis=0),
        jnp.concatenate([other, keep], axis=0),
    )

    outside = jnp.einsum(
        "tgn,ghnp->tghp", c, carried_in.reshape(G, per_group, state, width),
        preferred_element_type=f32,
    ).reshape(tokens, heads, width)
    mixed = inside + jnp.exp(within)[..., None] * outside + skip[None, :, None] * x.astype(f32)
    return mixed.astype(bf16).reshape(tokens, heads * width)


def solution(mesh):
    n_seq, n_head = mesh.devices.shape
    grid = Mesh(mesh.devices.reshape(n_seq, n_head // CORES, CORES), ("seq", "z", "core"))
    rows = P(("seq", "z", "core"), None)
    in_specs = (rows, rows, rows, rows, rows, P(("z", "core")))
    return jax.shard_map(local, mesh=grid, in_specs=in_specs, out_specs=rows, check_vma=False)
```

```python
import jax
import jax.numpy as jnp
from jax import lax
from jax.sharding import Mesh
from jax.sharding import PartitionSpec as P

G = 8
CORES = 2


def swap(value):
    return lax.ppermute(value, "core", [(0, 1), (1, 0)])


def split3(value):
    hi = lax.reduce_precision(value, exponent_bits=8, mantissa_bits=7)
    rest = value - hi
    mid = lax.reduce_precision(rest, exponent_bits=8, mantissa_bits=7)
    return jnp.stack([hi, mid, rest - mid], axis=-1).astype(jnp.bfloat16)


def join3(parts):
    parts = parts.astype(jnp.float32)
    return (parts[..., 0] + parts[..., 1]) + parts[..., 2]


def lower_mask(outs, ins):
    return (jnp.arange(ins)[None, :] < jnp.arange(outs)[:, None]).astype(jnp.float32)


def decay_matrix(totals, outs):
    count = totals.shape[0]
    a = jnp.arange(outs)[:, None, None]
    b = jnp.arange(count)[None, :, None]
    m = jnp.arange(count)[None, None, :]
    between = (b < m) & (m < a)
    exponent = jnp.sum(jnp.where(between[..., None], totals[None, None], 0.0), axis=2)
    exponent = exponent.transpose(2, 0, 1)
    earlier = (b < a)[None, :, :, 0]
    return jnp.where(earlier, jnp.exp(jnp.where(earlier, exponent, 0.0)), 0.0)


def local(features, increment_per_head, token_log_decay, b_matrix, c_matrix, skip_gain):
    f32, bf16 = jnp.float32, jnp.bfloat16
    n_seq = lax.axis_size("seq")
    n_z = lax.axis_size("z")
    n_core = lax.axis_size("core")
    z_idx = lax.axis_index("z")
    c_idx = lax.axis_index("core")
    tokens = features.shape[0]
    heads = increment_per_head.shape[1]
    width = features.shape[1] // heads
    state = b_matrix.shape[1] // G
    per_group = heads // G
    half = heads // n_core
    quarter = half // n_z

    x = features.reshape(tokens, heads, width)
    step = increment_per_head.astype(f32)
    within = jnp.cumsum(token_log_decay.astype(f32), axis=0)
    total = within[-1]
    b = b_matrix.reshape(tokens, G, state)
    c = c_matrix.reshape(tokens, G, state)
    partner = swap(jnp.concatenate([total, skip_gain.astype(f32)]))
    t_first = jnp.where(c_idx == 0, total, partner[:heads])
    t_second = jnp.where(c_idx == 0, partner[:heads], total)
    chip_skip = jnp.where(
        c_idx == 0,
        jnp.concatenate([skip_gain.astype(f32), partner[heads:]]),
        jnp.concatenate([partner[heads:], skip_gain.astype(f32)]),
    )

    factor = jnp.exp(total[None, :] - within) * step
    scaled = (x * factor[..., None]).astype(bf16)
    update = jnp.einsum(
        "sgn,sghp->ghnp", b, scaled.reshape(tokens, G, per_group, width),
        preferred_element_type=f32,
    ).reshape(heads, state, width)

    own = lax.dynamic_slice_in_dim(update, c_idx * half, half, 0)
    got = swap(lax.dynamic_slice_in_dim(update, (1 - c_idx) * half, half, 0))
    first = jnp.where(c_idx == 0, own, got)
    second = jnp.where(c_idx == 0, got, own)
    t_first = lax.dynamic_slice_in_dim(t_first, c_idx * half, half)
    t_second = lax.dynamic_slice_in_dim(t_second, c_idx * half, half)
    pair = jnp.exp(t_second)[:, None, None] * first + second

    pair = pair.astype(bf16).reshape(n_z, quarter, state, width)
    per_chip = chip_skip.shape[0]
    extra = jnp.concatenate(
        [
            split3((t_first + t_second).reshape(n_z, quarter)),
            jnp.broadcast_to(
                split3(chip_skip.reshape(quarter, per_chip // quarter)).reshape(1, quarter, -1),
                (n_z, quarter, 3 * per_chip // quarter),
            ),
        ],
        axis=-1,
    )
    extra = jnp.pad(
        extra, ((0, 0), (0, state - quarter), (0, width - extra.shape[-1]))
    )
    message = jnp.concatenate([pair, extra[:, None]], axis=1)
    rows = lax.all_to_all(message, "z", 0, 0, tiled=True)
    scores = jnp.einsum("tgn,sgn->gts", c, b, preferred_element_type=f32)
    scores = jnp.repeat(scores, per_group, axis=0)
    causal = (jnp.arange(tokens)[:, None] >= jnp.arange(tokens)[None, :])[None]
    w_t = within.T
    gap = w_t[:, :, None] - w_t[:, None, :]
    damping = jnp.where(causal, jnp.exp(jnp.where(causal, gap, 0.0)), 0.0)
    weight = (scores * damping * step.T[:, None, :]).astype(bf16)
    inside = jnp.einsum("hts,shp->thp", weight, x, preferred_element_type=f32)

    chip_totals = join3(rows[:, quarter, :quarter, 0:3])
    inside, chip_totals = lax.optimization_barrier((inside, chip_totals))
    skip = join3(
        rows[:, quarter, :quarter, 3 : 3 + 3 * per_chip // quarter].reshape(
            n_z, quarter, -1, 3
        )
    ).reshape(heads)
    scan = jnp.einsum(
        "hab,bhnp->ahnp",
        decay_matrix(chip_totals, n_z + 1),
        rows[:, :quarter].astype(f32),
        precision=lax.Precision.HIGHEST,
    )
    leads = jnp.einsum(
        "am,mh->ah", lower_mask(n_z + 1, n_z), chip_totals, precision=lax.Precision.HIGHEST
    )
    starts, run = scan[:n_z], scan[n_z]
    lead, before = leads[:n_z], leads[n_z]

    per = quarter * width // n_seq
    chunks = run.transpose(0, 2, 1).reshape(n_seq, per, state)
    row_totals = jnp.repeat(before, width).reshape(n_seq, per)
    packed = jnp.concatenate(
        [chunks, jnp.pad(row_totals, ((0, 0), (0, state - per)))[:, None, :]], axis=1
    )
    packed = jnp.pad(packed, ((0, 0), (0, -(per + 1) % 8), (0, 0)))
    gathered = lax.all_to_all(packed, "seq", 0, 0, tiled=True)
    entering = jnp.einsum(
        "rab,brn->arn",
        decay_matrix(gathered[:, per, :per], n_seq),
        gathered[:, :per],
        precision=lax.Precision.HIGHEST,
    )
    acc_s = lax.all_to_all(entering.astype(bf16), "seq", 0, 0, tiled=True).astype(f32)
    acc_s = acc_s.reshape(quarter, width, state).transpose(0, 2, 1)

    chip_in = starts + jnp.exp(lead)[:, :, None, None] * acc_s[None]
    back = lax.all_to_all(chip_in.astype(bf16), "z", 0, 0, tiled=True)
    entry = back.astype(f32).reshape(half, state, width)

    into_second = jnp.exp(t_first)[:, None, None] * entry + first
    keep = jnp.where(c_idx == 0, entry, into_second).astype(bf16)
    send = jnp.where(c_idx == 0, into_second, entry).astype(bf16)
    other = swap(send)
    carried_in = jnp.where(
        c_idx == 0,
        jnp.concatenate([keep, other], axis=0),
        jnp.concatenate([other, keep], axis=0),
    )

    outside = jnp.einsum(
        "tgn,ghnp->tghp", c, carried_in.reshape(G, per_group, state, width),
        preferred_element_type=f32,
    ).reshape(tokens, heads, width)
    mixed = inside + jnp.exp(within)[..., None] * outside + skip[None, :, None] * x.astype(f32)
    return mixed.astype(bf16).reshape(tokens, heads * width)


def solution(mesh):
    n_seq, n_head = mesh.devices.shape
    grid = Mesh(mesh.devices.reshape(n_seq, n_head // CORES, CORES), ("seq", "z", "core"))
    rows = P(("seq", "z", "core"), None)
    in_specs = (rows, rows, rows, rows, rows, P(("z", "core")))
    return jax.shard_map(local, mesh=grid, in_specs=in_specs, out_specs=rows, check_vma=False)
```

```python
import jax
import jax.numpy as jnp
from jax import lax
from jax.sharding import Mesh
from jax.sharding import PartitionSpec as P

G = 8
CORES = 2


def swap(value):
    return lax.ppermute(value, "core", [(0, 1), (1, 0)])


def split3(value):
    hi = lax.reduce_precision(value, exponent_bits=8, mantissa_bits=7)
    rest = value - hi
    mid = lax.reduce_precision(rest, exponent_bits=8, mantissa_bits=7)
    return jnp.stack([hi, mid, rest - mid], axis=-1).astype(jnp.bfloat16)


def join3(parts):
    parts = parts.astype(jnp.float32)
    return (parts[..., 0] + parts[..., 1]) + parts[..., 2]


def lower_mask(outs, ins):
    return (jnp.arange(ins)[None, :] < jnp.arange(outs)[:, None]).astype(jnp.float32)


def decay_matrix(totals, outs):
    count = totals.shape[0]
    a = jnp.arange(outs)[:, None, None]
    b = jnp.arange(count)[None, :, None]
    m = jnp.arange(count)[None, None, :]
    between = ((b < m) & (m < a)).astype(jnp.float32)
    exponent = jnp.einsum("abm,mh->hab", between, totals, precision=lax.Precision.HIGHEST)
    earlier = (b < a)[None, :, :, 0]
    return jnp.where(earlier, jnp.exp(jnp.where(earlier, exponent, 0.0)), 0.0)


def local(features, increment_per_head, token_log_decay, b_matrix, c_matrix, skip_gain):
    f32, bf16 = jnp.float32, jnp.bfloat16
    n_seq = lax.axis_size("seq")
    n_z = lax.axis_size("z")
    n_core = lax.axis_size("core")
    z_idx = lax.axis_index("z")
    c_idx = lax.axis_index("core")
    tokens = features.shape[0]
    heads = increment_per_head.shape[1]
    width = features.shape[1] // heads
    state = b_matrix.shape[1] // G
    per_group = heads // G
    half = heads // n_core
    quarter = half // n_z

    x = features.reshape(tokens, heads, width)
    step = increment_per_head.astype(f32)
    within = jnp.cumsum(token_log_decay.astype(f32), axis=0)
    total = within[-1]
    b = b_matrix.reshape(tokens, G, state)
    c = c_matrix.reshape(tokens, G, state)
    partner = swap(jnp.concatenate([total, skip_gain.astype(f32)]))
    t_first = jnp.where(c_idx == 0, total, partner[:heads])
    t_second = jnp.where(c_idx == 0, partner[:heads], total)
    chip_skip = jnp.where(
        c_idx == 0,
        jnp.concatenate([skip_gain.astype(f32), partner[heads:]]),
        jnp.concatenate([partner[heads:], skip_gain.astype(f32)]),
    )

    factor = jnp.exp(total[None, :] - within) * step
    scaled = (x * factor[..., None]).astype(bf16)
    update = jnp.einsum(
        "sgn,sghp->ghnp", b, scaled.reshape(tokens, G, per_group, width),
        preferred_element_type=f32,
    ).reshape(heads, state, width)

    own = lax.dynamic_slice_in_dim(update, c_idx * half, half, 0)
    got = swap(lax.dynamic_slice_in_dim(update, (1 - c_idx) * half, half, 0))
    first = jnp.where(c_idx == 0, own, got)
    second = jnp.where(c_idx == 0, got, own)
    t_first = lax.dynamic_slice_in_dim(t_first, c_idx * half, half)
    t_second = lax.dynamic_slice_in_dim(t_second, c_idx * half, half)
    pair = jnp.exp(t_second)[:, None, None] * first + second

    pair = pair.astype(bf16).reshape(n_z, quarter, state, width)
    per_chip = chip_skip.shape[0]
    extra = jnp.concatenate(
        [
            split3((t_first + t_second).reshape(n_z, quarter)),
            jnp.broadcast_to(
                split3(chip_skip.reshape(quarter, per_chip // quarter)).reshape(1, quarter, -1),
                (n_z, quarter, 3 * per_chip // quarter),
            ),
        ],
        axis=-1,
    )
    extra = jnp.pad(
        extra, ((0, 0), (0, state - quarter), (0, width - extra.shape[-1]))
    )
    message = jnp.concatenate([pair, extra[:, None]], axis=1)
    rows = lax.all_to_all(message, "z", 0, 0, tiled=True)
    scores = jnp.einsum("tgn,sgn->gts", c, b, preferred_element_type=f32)
    scores = jnp.repeat(scores, per_group, axis=0)
    causal = (jnp.arange(tokens)[:, None] >= jnp.arange(tokens)[None, :])[None]
    w_t = within.T
    gap = w_t[:, :, None] - w_t[:, None, :]
    damping = jnp.where(causal, jnp.exp(jnp.where(causal, gap, 0.0)), 0.0)
    weight = (scores * damping * step.T[:, None, :]).astype(bf16)
    inside = jnp.einsum("hts,shp->thp", weight, x, preferred_element_type=f32)

    chip_totals = join3(rows[:, quarter, :quarter, 0:3])
    inside, chip_totals = lax.optimization_barrier((inside, chip_totals))
    skip = join3(
        rows[:, quarter, :quarter, 3 : 3 + 3 * per_chip // quarter].reshape(
            n_z, quarter, -1, 3
        )
    ).reshape(heads)
    scan = jnp.einsum(
        "hab,bhnp->ahnp",
        decay_matrix(chip_totals, n_z + 1),
        rows[:, :quarter].astype(f32),
        precision=lax.Precision.HIGHEST,
    )
    leads = jnp.einsum(
        "am,mh->ah", lower_mask(n_z + 1, n_z), chip_totals, precision=lax.Precision.HIGHEST
    )
    starts, run = scan[:n_z], scan[n_z]
    lead, before = leads[:n_z], leads[n_z]

    per = quarter * width // n_seq
    chunks = run.transpose(0, 2, 1).reshape(n_seq, per, state)
    row_totals = jnp.repeat(before, width).reshape(n_seq, per)
    totals3 = split3(row_totals).transpose(0, 2, 1)
    packed = jnp.concatenate(
        [chunks.astype(bf16), jnp.pad(totals3, ((0, 0), (0, 0), (0, state - per)))], axis=1
    )
    packed = jnp.pad(packed, ((0, 0), (0, -(per + 3) % 16), (0, 0)))
    gathered = lax.all_to_all(packed, "seq", 0, 0, tiled=True)
    entering = jnp.einsum(
        "rab,brn->arn",
        decay_matrix(join3(gathered[:, per : per + 3, :per].transpose(0, 2, 1)), n_seq),
        gathered[:, :per].astype(f32),
        precision=lax.Precision.HIGHEST,
    )
    acc_s = lax.all_to_all(entering.astype(bf16), "seq", 0, 0, tiled=True).astype(f32)
    acc_s = acc_s.reshape(quarter, width, state).transpose(0, 2, 1)

    chip_in = starts + jnp.exp(lead)[:, :, None, None] * acc_s[None]
    back = lax.all_to_all(chip_in.astype(bf16), "z", 0, 0, tiled=True)
    entry = back.astype(f32).reshape(half, state, width)

    into_second = jnp.exp(t_first)[:, None, None] * entry + first
    keep = jnp.where(c_idx == 0, entry, into_second).astype(bf16)
    send = jnp.where(c_idx == 0, into_second, entry).astype(bf16)
    other = swap(send)
    carried_in = jnp.where(
        c_idx == 0,
        jnp.concatenate([keep, other], axis=0),
        jnp.concatenate([other, keep], axis=0),
    )

    outside = jnp.einsum(
        "tgn,ghnp->tghp", c, carried_in.reshape(G, per_group, state, width),
        preferred_element_type=f32,
    ).reshape(tokens, heads, width)
    mixed = inside + jnp.exp(within)[..., None] * outside + skip[None, :, None] * x.astype(f32)
    return mixed.astype(bf16).reshape(tokens, heads * width)


def solution(mesh):
    n_seq, n_head = mesh.devices.shape
    grid = Mesh(mesh.devices.reshape(n_seq, n_head // CORES, CORES), ("seq", "z", "core"))
    rows = P(("seq", "z", "core"), None)
    in_specs = (rows, rows, rows, rows, rows, P(("z", "core")))
    return jax.shard_map(local, mesh=grid, in_specs=in_specs, out_specs=rows, check_vma=False)
```
